256 devices in a mesh: mode: 8 (over z), row: 8 (over y, x_hi), col: 4 (over x_lo, core).
Axes of the slice: x: 4 (x_hi: 2, x_lo: 2; x = x_hi * 2 + x_lo), y: 4, z: 8, core: 2. Of those that a mesh axis runs over, the one named last changes fastest.
Arguments:
- coords: float32 [2, 32768], replicated, may hold values from 0 to 1
- wave: float32 [2, 4096], replicated, may hold values from -60 to 60
- col_factor: bfloat16 [2, 4096, 1024], P(None, 'mode', 'col'), may hold values from -0.011962891 to 0.011962891
- counts: int32 [64], replicated, may hold values from 1 to 8, as said below
- blocks: int32 [2], replicated, may hold values from 0 to 63, as said below
- inverse_first: float32 [512, 512], replicated, may hold values from -1 to 3, as said below
- inverse_second: float32 [512, 512], replicated, may hold values from -1 to 3, as said below
Outputs:
- factored: float32 [32768, 1024], P(('mode', 'row'), 'col')
The draws below stay inside these ranges and needn't reach their ends.
Inputs may be any that keep to these rules, and one draw needn't show every extreme that they name: `counts`: some block has 8 nodes and some block has 1. `blocks`: the two indices differ, and one of them is the last block. `inverse_first`: diagonal entries from 1.5 to 2.5; the other entries independent, each under 0.75 in magnitude. `inverse_second`: diagonal entries from 1.5 to 2.5; the other entries independent, each under 0.75 in magnitude.
All inputs are finite; a program needn't handle non-finite values.
Results may differ from the reference program's by a relative error of at most 0.00073.
Values may be sent and summed in bfloat16 or wider, within the bound.
No kernel may reach another device: no remote copies, remote signals or barrier semaphores. Data moves between devices by JAX's collectives and lax.ppermute only.
A program may use at most 64 MiB of HBM per device.

```python
import jax
import jax.numpy as jnp
from jax import lax

M = 4096
BS = 512
QMAX = 8
ROWS = 32768
NBLK = 64


def draw_counts(key, part):
    first, second, third = jax.random.split(jax.random.fold_in(key, 11), 3)
    values = jax.random.randint(first, (NBLK,), 1, QMAX + 1)
    place = jax.random.randint(second, (), 0, NBLK)
    other = (place + 1 + jax.random.randint(third, (), 0, NBLK - 1)) % NBLK
    index = jnp.arange(NBLK)
    values = jnp.where(index == place, QMAX, values)
    values = jnp.where(index == other, 1, values)
    return values.astype(jnp.int32)


def draw_blocks(key, part):
    first, second = jax.random.split(jax.random.fold_in(key, 13), 2)
    other = jax.random.randint(first, (), 0, NBLK - 1)
    last_block = jnp.int32(NBLK - 1)
    flip = jax.random.randint(second, (), 0, 2)
    lead = jnp.where(flip == 0, other, last_block)
    follow = jnp.where(flip == 0, last_block, other)
    return jnp.stack([lead, follow]).astype(jnp.int32)


def inverse_draw(key):
    first = jax.random.fold_in(key, 0)
    spread = 0.5 / BS ** 0.5
    eye_mask = jnp.eye(BS, dtype=jnp.float32)
    off = jnp.clip(jax.random.normal(first, (BS, BS), jnp.float32), -6.0, 6.0) * spread
    diag = jnp.full((BS, 1), 2.0, jnp.float32)
    return (off * (1.0 - eye_mask) + diag * eye_mask).astype(jnp.float32)


def draw_inverse_first(key, part):
    return inverse_draw(jax.random.fold_in(key, 17))


def draw_inverse_second(key, part):
    return inverse_draw(jax.random.fold_in(key, 19))


def levels(key, dims, cuts, low, largest):
    level = 1.0
    for axis_at, parts in cuts:
        steps = jax.random.uniform(jax.random.fold_in(jax.random.fold_in(key, 6), axis_at), (parts,), jnp.float32, low / len(cuts), largest / len(cuts))
        level = level * jnp.repeat(jnp.exp(steps), dims[axis_at] // parts).reshape((-1,) + (1,) * (len(dims) - 1 - axis_at))
    return level


def gaussian(key, shape, scale, most, pieces=(), held_as=jnp.bfloat16):
    entries = jax.random.normal(key, shape, jnp.float32) * scale
    if len(pieces) > 0:
        entries = levels(key, shape, pieces, -0.22, 0.18) * entries
    return jnp.clip(entries, min=-most, max=most).astype(held_as)


def setup_inputs(seed: int = 0) -> dict:
    seeds = jax.random.split(jax.random.key(seed), 8)
    return {
        "coords": jnp.clip(jax.random.uniform(seeds[0], (2, ROWS), jnp.float32, 0.0, 1.0), 0.0, 1.0),
        "wave": jnp.clip(jax.random.uniform(seeds[1], (2, M), jnp.float32, -60.0, 60.0), -60.0, 60.0),
        "col_factor": gaussian(seeds[2], (2, M, 2 * BS), 0.002, 0.011962891, ((1, 8), (2, 4))),
        "counts": draw_counts(jax.random.fold_in(seeds[7], 71), 0),
        "blocks": draw_blocks(jax.random.fold_in(seeds[7], 71), 0),
        "inverse_first": draw_inverse_first(jax.random.fold_in(seeds[7], 71), 0),
        "inverse_second": draw_inverse_second(jax.random.fold_in(seeds[7], 71), 0),
    }


screen_rate = 6.0
bloch_phase = 0.7
real_amplitude = 0.15
identity_weight = 0.5


def make_waves(xr, yr, kvec):
    theta = xr[:, None] * kvec[0][None, :] + yr[:, None] * kvec[1][None, :]
    return jnp.concatenate([jnp.cos(theta), -jnp.sin(theta)], axis=1).astype(jnp.bfloat16)


def real_part(xr, yr, xc, yc):
    dx = xr[:, None] - xc[None, :]
    dy = yr[:, None] - yc[None, :]
    total = jnp.zeros(dx.shape, jnp.float32)
    for shift in (-1, 0, 1):
        total = total + jnp.cos(jnp.float32(bloch_phase * shift)) * jnp.exp(-screen_rate * ((dx - shift) ** 2 + dy * dy))
    return total


def reference(coords, wave, col_factor, counts, blocks, inverse_first, inverse_second):
    factor_flat = col_factor.reshape(2 * M, 2 * BS)
    columns = jnp.arange(2 * BS, dtype=jnp.int32)
    points = jnp.take(blocks, columns // BS) * BS + columns % BS
    xc = jnp.take(coords[0], points)
    yc = jnp.take(coords[1], points)
    scales = counts.astype(jnp.float32) / QMAX
    step_rows = min(ROWS, 1024)

    def fill(start):
        rows = start + jnp.arange(step_rows, dtype=jnp.int32)
        xr = lax.dynamic_slice_in_dim(coords[0], start, step_rows, 0)
        yr = lax.dynamic_slice_in_dim(coords[1], start, step_rows, 0)
        spectral = jnp.dot(make_waves(xr, yr, wave), factor_flat, preferred_element_type=jnp.float32)
        scale_rows = jnp.take(scales, rows // BS)
        tile = real_amplitude * scale_rows[:, None] * real_part(xr, yr, xc, yc)
        diag = jnp.where(rows[:, None] == points[None, :], jnp.float32(identity_weight), jnp.float32(0.0))
        return spectral + tile + diag

    starts = jnp.arange(ROWS // step_rows, dtype=jnp.int32) * step_rows
    panel = lax.map(fill, starts).reshape(ROWS, 2 * BS)
    highest = lax.Precision.HIGHEST
    first = panel[:, :BS]
    second = panel[:, BS:]
    lower_first = jnp.dot(first, inverse_first, precision=highest, preferred_element_type=jnp.float32)
    pivot = lax.dynamic_slice_in_dim(second, (blocks[0] * BS).astype(jnp.int32), BS, 0)
    schur = second - jnp.dot(lower_first, pivot, precision=highest, preferred_element_type=jnp.float32)
    lower_second = jnp.dot(schur, inverse_second, precision=highest, preferred_element_type=jnp.float32)
    return jnp.concatenate([lower_first, lower_second], axis=1)
```

```python
import jax
import jax.numpy as jnp
from jax import lax
from jax.sharding import PartitionSpec as P

QMAX = 8


screen_rate = 6.0
bloch_phase = 0.7
real_amplitude = 0.15
identity_weight = 0.5

HIGHEST = lax.Precision.HIGHEST


def real_part(xr, yr, xc, yc):
    dx = xr[:, None] - xc[None, :]
    dy = yr[:, None] - yc[None, :]
    total = jnp.zeros(dx.shape, jnp.float32)
    for shift in (-1, 0, 1):
        total = total + jnp.cos(jnp.float32(bloch_phase * shift)) * jnp.exp(
            -screen_rate * ((dx - shift) ** 2 + dy * dy)
        )
    return total


def spectral_rows(xr, yr, wave, factor):
    theta = xr[:, None] * wave[0][None, :] + yr[:, None] * wave[1][None, :]
    cos_part = jnp.cos(theta).astype(jnp.bfloat16)
    sin_part = (-jnp.sin(theta)).astype(jnp.bfloat16)
    cos_part, sin_part = lax.optimization_barrier((cos_part, sin_part))
    spec = jnp.dot(cos_part, factor[0], preferred_element_type=jnp.float32)
    return spec + jnp.dot(sin_part, factor[1], preferred_element_type=jnp.float32)


def panel_rows(start, count, scale, coords, wave, factor, xc, yc, points):
    rows = start + jnp.arange(count, dtype=jnp.int32)
    xr = lax.dynamic_slice_in_dim(coords[0], start, count, 0)
    yr = lax.dynamic_slice_in_dim(coords[1], start, count, 0)
    spectral = spectral_rows(xr, yr, wave, factor)
    tile = real_amplitude * scale * real_part(xr, yr, xc, yc)
    diag = jnp.where(
        rows[:, None] == points[None, :], jnp.float32(identity_weight), jnp.float32(0.0)
    )
    return spectral + tile + diag


def mm(a, b):
    return jnp.dot(a, b, precision=HIGHEST, preferred_element_type=jnp.float32)


def on_device(coords, wave, col_factor, counts, blocks, inverse_first, inverse_second):
    row_count = lax.axis_size("row")
    mode_index = lax.axis_index("mode")
    row_index = lax.axis_index("row")
    col_index = lax.axis_index("col")
    block = inverse_first.shape[0]
    width = col_factor.shape[2]
    rows_dev = coords.shape[1] // (lax.axis_size("mode") * row_count)
    assert rows_dev == block and 2 * width == block
    group = mode_index * row_count + row_index

    factor = lax.all_gather(col_factor, "mode", axis=1, tiled=True)

    half = col_index % 2
    col_start = jnp.take(blocks, col_index // 2) * block + half * width
    points = col_start + jnp.arange(width, dtype=jnp.int32)
    xc = lax.dynamic_slice_in_dim(coords[0], col_start, width, 0)
    yc = lax.dynamic_slice_in_dim(coords[1], col_start, width, 0)

    own_start = group * rows_dev
    own_scale = jnp.take(counts, group).astype(jnp.float32) / QMAX
    panel_own = panel_rows(own_start, rows_dev, own_scale, coords, wave, factor, xc, yc, points)

    pivot_block = blocks[0]
    chunk = block // row_count
    pivot_scale = jnp.take(counts, pivot_block).astype(jnp.float32) / QMAX
    pivot_chunk = panel_rows(
        pivot_block * block + row_index * chunk, chunk, pivot_scale, coords, wave, factor, xc, yc, points
    )
    pivot_mine = lax.all_gather(pivot_chunk, "row", axis=0, tiled=True)

    swap = [(0, 1), (1, 0), (2, 3), (3, 2)]
    other = lax.ppermute(panel_own, "col", swap)
    pivot_other = lax.ppermute(pivot_mine, "col", [(2, 3), (3, 2)])
    first_a = lax.ppermute(panel_own, "col", [(0, 2), (1, 3)])
    first_b = lax.ppermute(panel_own, "col", [(0, 3), (1, 2)])

    s_mine = half * width
    s_other = width - s_mine
    out_cols = half * width

    def rows_of(mat, start):
        return lax.dynamic_slice_in_dim(mat, start, width, 0)

    def left_side():
        inv = lax.dynamic_slice_in_dim(inverse_first, out_cols, width, 1)
        return mm(panel_own, rows_of(inv, s_mine)) + mm(other, rows_of(inv, s_other))

    def right_side():
        inv = lax.dynamic_slice_in_dim(inverse_second, out_cols, width, 1)
        q = mm(pivot_mine, rows_of(inv, s_mine)) + mm(pivot_other, rows_of(inv, s_other))
        z = mm(inverse_first, q)
        direct = mm(panel_own, rows_of(inv, s_mine)) + mm(other, rows_of(inv, s_other))
        s_a = s_mine
        s_b = width - s_a
        correction = mm(first_a, rows_of(z, s_a)) + mm(first_b, rows_of(z, s_b))
        return direct - correction

    return lax.cond(col_index < 2, left_side, right_side)


def solution(mesh):
    return jax.shard_map(
        on_device,
        mesh=mesh,
        in_specs=(P(), P(), P(None, "mode", "col"), P(), P(), P(), P()),
        out_specs=P(("mode", "row"), "col"),
        check_vma=False,
    )
```

```python
import jax
import jax.numpy as jnp
from jax import lax
from jax.sharding import PartitionSpec as P

QMAX = 8


screen_rate = 6.0
bloch_phase = 0.7
real_amplitude = 0.15
identity_weight = 0.5

HIGHEST = lax.Precision.HIGHEST


def real_part(xr, yr, xc, yc):
    dx = xr[:, None] - xc[None, :]
    dy = yr[:, None] - yc[None, :]
    total = jnp.zeros(dx.shape, jnp.float32)
    for shift in (-1, 0, 1):
        total = total + jnp.cos(jnp.float32(bloch_phase * shift)) * jnp.exp(
            -screen_rate * ((dx - shift) ** 2 + dy * dy)
        )
    return total


def spectral_rows(xr, yr, wave, factor):
    theta = xr[:, None] * wave[0][None, :] + yr[:, None] * wave[1][None, :]
    cos_part = jnp.cos(theta).astype(jnp.bfloat16)
    sin_part = (-jnp.sin(theta)).astype(jnp.bfloat16)
    cos_part, sin_part = lax.optimization_barrier((cos_part, sin_part))
    spec = jnp.dot(cos_part, factor[0], preferred_element_type=jnp.float32)
    return spec + jnp.dot(sin_part, factor[1], preferred_element_type=jnp.float32)


def panel_rows(start, count, scale, coords, wave, factor, xc, yc, points):
    rows = start + jnp.arange(count, dtype=jnp.int32)
    xr = lax.dynamic_slice_in_dim(coords[0], start, count, 0)
    yr = lax.dynamic_slice_in_dim(coords[1], start, count, 0)
    spectral = spectral_rows(xr, yr, wave, factor)
    tile = real_amplitude * scale * real_part(xr, yr, xc, yc)
    diag = jnp.where(
        rows[:, None] == points[None, :], jnp.float32(identity_weight), jnp.float32(0.0)
    )
    return spectral + tile + diag


def mm(a, b):
    return jnp.dot(a, b, precision=HIGHEST, preferred_element_type=jnp.float32)


def on_device(coords, wave, col_factor, counts, blocks, inverse_first, inverse_second):
    row_count = lax.axis_size("row")
    mode_index = lax.axis_index("mode")
    row_index = lax.axis_index("row")
    col_index = lax.axis_index("col")
    block = inverse_first.shape[0]
    width = col_factor.shape[2]
    rows_dev = coords.shape[1] // (lax.axis_size("mode") * row_count)
    assert rows_dev == block and 2 * width == block
    group = mode_index * row_count + row_index

    factor = lax.all_gather(col_factor, "mode", axis=1, tiled=True)

    half = col_index % 2
    col_start = jnp.take(blocks, col_index // 2) * block + half * width
    points = col_start + jnp.arange(width, dtype=jnp.int32)
    xc = lax.dynamic_slice_in_dim(coords[0], col_start, width, 0)
    yc = lax.dynamic_slice_in_dim(coords[1], col_start, width, 0)

    own_start = group * rows_dev
    own_scale = jnp.take(counts, group).astype(jnp.float32) / QMAX
    panel_own = panel_rows(own_start, rows_dev, own_scale, coords, wave, factor, xc, yc, points)

    pivot_block = blocks[0]
    pivot_start = pivot_block * block
    local_modes = col_factor.shape[1]
    local_wave = lax.dynamic_slice_in_dim(wave, mode_index * local_modes, local_modes, 1)
    xp = lax.dynamic_slice_in_dim(coords[0], pivot_start, block, 0)
    yp = lax.dynamic_slice_in_dim(coords[1], pivot_start, block, 0)
    pivot_spectral = lax.psum(spectral_rows(xp, yp, local_wave, col_factor), "mode")
    pivot_scale = jnp.take(counts, pivot_block).astype(jnp.float32) / QMAX
    pivot_rows_idx = pivot_start + jnp.arange(block, dtype=jnp.int32)
    pivot_mine = (
        pivot_spectral
        + real_amplitude * pivot_scale * real_part(xp, yp, xc, yc)
        + jnp.where(
            pivot_rows_idx[:, None] == points[None, :],
            jnp.float32(identity_weight),
            jnp.float32(0.0),
        )
    )

    swap = [(0, 1), (1, 0), (2, 3), (3, 2)]
    right_swap = [(2, 3), (3, 2)]
    other = lax.ppermute(panel_own, "col", swap)
    pivot_other = lax.ppermute(pivot_mine, "col", right_swap)
    first_a = lax.ppermute(panel_own, "col", [(0, 2), (1, 3)])
    first_b = lax.ppermute(first_a, "col", right_swap)

    s_mine = half * width
    s_other = width - s_mine
    out_cols = half * width

    def rows_of(mat, start):
        return lax.dynamic_slice_in_dim(mat, start, width, 0)

    def left_side():
        inv = lax.dynamic_slice_in_dim(inverse_first, out_cols, width, 1)
        return mm(panel_own, rows_of(inv, s_mine)) + mm(other, rows_of(inv, s_other))

    def right_side():
        inv = lax.dynamic_slice_in_dim(inverse_second, out_cols, width, 1)
        q = mm(pivot_mine, rows_of(inv, s_mine)) + mm(pivot_other, rows_of(inv, s_other))
        z = mm(inverse_first, q)
        direct = mm(panel_own, rows_of(inv, s_mine)) + mm(other, rows_of(inv, s_other))
        correction = mm(first_a, rows_of(z, s_mine)) + mm(first_b, rows_of(z, s_other))
        return direct - correction

    return lax.cond(col_index < 2, left_side, right_side)


def solution(mesh):
    return jax.shard_map(
        on_device,
        mesh=mesh,
        in_specs=(P(), P(), P(None, "mode", "col"), P(), P(), P(), P()),
        out_specs=P(("mode", "row"), "col"),
        check_vma=False,
    )
```

```python
import jax
import jax.numpy as jnp
from jax import lax
from jax.sharding import PartitionSpec as P

QMAX = 8


screen_rate = 6.0
bloch_phase = 0.7
real_amplitude = 0.15
identity_weight = 0.5

HIGHEST = lax.Precision.HIGHEST


def real_part(xr, yr, xc, yc):
    dx = xr[:, None] - xc[None, :]
    dy = yr[:, None] - yc[None, :]
    total = jnp.zeros(dx.shape, jnp.float32)
    for shift in (-1, 0, 1):
        total = total + jnp.cos(jnp.float32(bloch_phase * shift)) * jnp.exp(
            -screen_rate * ((dx - shift) ** 2 + dy * dy)
        )
    return total


def spectral_rows(xr, yr, wave, factor):
    theta = xr[:, None] * wave[0][None, :] + yr[:, None] * wave[1][None, :]
    cos_part = jnp.cos(theta).astype(jnp.bfloat16)
    sin_part = (-jnp.sin(theta)).astype(jnp.bfloat16)
    cos_part, sin_part = lax.optimization_barrier((cos_part, sin_part))
    spec = jnp.dot(cos_part, factor[0], preferred_element_type=jnp.float32)
    return spec + jnp.dot(sin_part, factor[1], preferred_element_type=jnp.float32)


def panel_rows(start, count, scale, coords, wave, factor, xc, yc, points):
    rows = start + jnp.arange(count, dtype=jnp.int32)
    xr = lax.dynamic_slice_in_dim(coords[0], start, count, 0)
    yr = lax.dynamic_slice_in_dim(coords[1], start, count, 0)
    spectral = spectral_rows(xr, yr, wave, factor)
    tile = real_amplitude * scale * real_part(xr, yr, xc, yc)
    diag = jnp.where(
        rows[:, None] == points[None, :], jnp.float32(identity_weight), jnp.float32(0.0)
    )
    return spectral + tile + diag


def mm(a, b):
    return jnp.dot(a, b, precision=HIGHEST, preferred_element_type=jnp.float32)


def on_device(coords, wave, col_factor, counts, blocks, inverse_first, inverse_second):
    row_count = lax.axis_size("row")
    mode_index = lax.axis_index("mode")
    row_index = lax.axis_index("row")
    col_index = lax.axis_index("col")
    block = inverse_first.shape[0]
    width = col_factor.shape[2]
    rows_dev = coords.shape[1] // (lax.axis_size("mode") * row_count)
    assert rows_dev == block and 2 * width == block
    group = mode_index * row_count + row_index

    factor = lax.all_gather(col_factor, "mode", axis=1, tiled=True)

    half = col_index % 2
    col_start = jnp.take(blocks, col_index // 2) * block + half * width
    points = col_start + jnp.arange(width, dtype=jnp.int32)
    xc = lax.dynamic_slice_in_dim(coords[0], col_start, width, 0)
    yc = lax.dynamic_slice_in_dim(coords[1], col_start, width, 0)

    own_start = group * rows_dev
    own_scale = jnp.take(counts, group).astype(jnp.float32) / QMAX
    panel_own = panel_rows(own_start, rows_dev, own_scale, coords, wave, factor, xc, yc, points)

    pivot_block = blocks[0]
    chunk = block // lax.axis_size("mode")
    pivot_scale = jnp.take(counts, pivot_block).astype(jnp.float32) / QMAX
    pivot_chunk = panel_rows(
        pivot_block * block + mode_index * chunk, chunk, pivot_scale, coords, wave, factor, xc, yc, points
    )
    pivot_mine = lax.all_gather(pivot_chunk, "mode", axis=0, tiled=True)

    swap = [(0, 1), (1, 0), (2, 3), (3, 2)]
    right_swap = [(2, 3), (3, 2)]
    other = lax.ppermute(panel_own, "col", swap)
    pivot_other = lax.ppermute(pivot_mine, "col", right_swap)
    first_a = lax.ppermute(panel_own, "col", [(0, 2), (1, 3)])
    first_b = lax.ppermute(first_a, "col", right_swap)

    s_mine = half * width
    s_other = width - s_mine
    out_cols = half * width

    def rows_of(mat, start):
        return lax.dynamic_slice_in_dim(mat, start, width, 0)

    def left_side():
        inv = lax.dynamic_slice_in_dim(inverse_first, out_cols, width, 1)
        return mm(panel_own, rows_of(inv, s_mine)) + mm(other, rows_of(inv, s_other))

    def right_side():
        inv = lax.dynamic_slice_in_dim(inverse_second, out_cols, width, 1)
        q = mm(pivot_mine, rows_of(inv, s_mine)) + mm(pivot_other, rows_of(inv, s_other))
        z = mm(inverse_first, q)
        direct = mm(panel_own, rows_of(inv, s_mine)) + mm(other, rows_of(inv, s_other))
        correction = mm(first_a, rows_of(z, s_mine)) + mm(first_b, rows_of(z, s_other))
        return direct - correction

    return lax.cond(col_index < 2, left_side, right_side)


def solution(mesh):
    return jax.shard_map(
        on_device,
        mesh=mesh,
        in_specs=(P(), P(), P(None, "mode", "col"), P(), P(), P(), P()),
        out_specs=P(("mode", "row"), "col"),
        check_vma=False,
    )
```

```python
import jax
import jax.numpy as jnp
from jax import lax
from jax.sharding import PartitionSpec as P

QMAX = 8


screen_rate = 6.0
bloch_phase = 0.7
real_amplitude = 0.15
identity_weight = 0.5

HIGHEST = lax.Precision.HIGHEST


def real_part(xr, yr, xc, yc):
    dx = xr[:, None] - xc[None, :]
    dy = yr[:, None] - yc[None, :]
    total = jnp.zeros(dx.shape, jnp.float32)
    for shift in (-1, 0, 1):
        total = total + jnp.cos(jnp.float32(bloch_phase * shift)) * jnp.exp(
            -screen_rate * ((dx - shift) ** 2 + dy * dy)
        )
    return total


def make_waves(xr, yr, kvec):
    theta = xr[:, None] * kvec[0][None, :] + yr[:, None] * kvec[1][None, :]
    cos_part = jnp.cos(theta).astype(jnp.bfloat16)
    sin_part = (-jnp.sin(theta)).astype(jnp.bfloat16)
    return lax.optimization_barrier((cos_part, sin_part))


def wave_product(waves, factor):
    cos_part, sin_part = waves
    spec = jnp.dot(cos_part, factor[0], preferred_element_type=jnp.float32)
    return spec + jnp.dot(sin_part, factor[1], preferred_element_type=jnp.float32)


def ring_gather(x, axis, n, split_axis):
    fwd = [(i, (i + 1) % n) for i in range(n)]
    bwd = [(i, (i - 1) % n) for i in range(n)]
    pieces = [(0, x, None)]
    ahead, behind = x, x
    far = n // 2
    for step in range(1, far + 1):
        if step < far or n % 2 == 1:
            behind = lax.ppermute(behind, axis, fwd)
            ahead = lax.ppermute(ahead, axis, bwd)
            pieces.append((-step, behind, None))
            pieces.append((step, ahead, None))
        else:
            size = x.shape[split_axis] // 2
            lo = lax.slice_in_dim(behind, 0, size, axis=split_axis)
            hi = lax.slice_in_dim(ahead, size, 2 * size, axis=split_axis)
            pieces.append((step, lax.ppermute(lo, axis, fwd), 0))
            pieces.append((step, lax.ppermute(hi, axis, bwd), 1))
    return pieces


def mm(a, b):
    return jnp.dot(a, b, precision=HIGHEST, preferred_element_type=jnp.float32)


def on_device(coords, wave, col_factor, counts, blocks, inverse_first, inverse_second):
    mode_count = lax.axis_size("mode")
    row_count = lax.axis_size("row")
    mode_index = lax.axis_index("mode")
    row_index = lax.axis_index("row")
    col_index = lax.axis_index("col")
    block = inverse_first.shape[0]
    width = col_factor.shape[2]
    local_modes = col_factor.shape[1]
    rows_dev = coords.shape[1] // (mode_count * row_count)
    assert rows_dev == block and 2 * width == block and block % mode_count == 0
    group = mode_index * row_count + row_index

    half = col_index % 2
    col_start = jnp.take(blocks, col_index // 2) * block + half * width
    points = col_start + jnp.arange(width, dtype=jnp.int32)
    xc = lax.dynamic_slice_in_dim(coords[0], col_start, width, 0)
    yc = lax.dynamic_slice_in_dim(coords[1], col_start, width, 0)

    own_start = group * rows_dev
    xr = lax.dynamic_slice_in_dim(coords[0], own_start, rows_dev, 0)
    yr = lax.dynamic_slice_in_dim(coords[1], own_start, rows_dev, 0)

    pivot_block = blocks[0]
    chunk = block // mode_count
    pivot_chunk_start = pivot_block * block + mode_index * chunk
    xp = lax.dynamic_slice_in_dim(coords[0], pivot_chunk_start, chunk, 0)
    yp = lax.dynamic_slice_in_dim(coords[1], pivot_chunk_start, chunk, 0)

    spectral = jnp.zeros((rows_dev, width), jnp.float32)
    pivot_spectral = jnp.zeros((chunk, width), jnp.float32)
    for offset, piece, part in ring_gather(col_factor, "mode", mode_count, 1):
        source = (mode_index + offset) % mode_count
        count = piece.shape[1]
        first_mode = source * local_modes + (0 if part is None else part * count)
        kvec = lax.dynamic_slice_in_dim(wave, first_mode, count, 1)
        spectral = spectral + wave_product(make_waves(xr, yr, kvec), piece)
        pivot_spectral = pivot_spectral + wave_product(make_waves(xp, yp, kvec), piece)

    own_rows = own_start + jnp.arange(rows_dev, dtype=jnp.int32)
    own_scale = jnp.take(counts, group).astype(jnp.float32) / QMAX
    panel_own = (
        spectral
        + real_amplitude * own_scale * real_part(xr, yr, xc, yc)
        + jnp.where(own_rows[:, None] == points[None, :], jnp.float32(identity_weight), jnp.float32(0.0))
    )
    pivot_rows = pivot_chunk_start + jnp.arange(chunk, dtype=jnp.int32)
    pivot_scale = jnp.take(counts, pivot_block).astype(jnp.float32) / QMAX
    pivot_chunk = (
        pivot_spectral
        + real_amplitude * pivot_scale * real_part(xp, yp, xc, yc)
        + jnp.where(pivot_rows[:, None] == points[None, :], jnp.float32(identity_weight), jnp.float32(0.0))
    )

    by_offset = {}
    for offset, piece, part in ring_gather(pivot_chunk, "mode", mode_count, 0):
        by_offset.setdefault(offset % mode_count, []).append((-1 if part is None else part, piece))
    stacked = jnp.concatenate(
        [jnp.concatenate([p for _, p in sorted(by_offset[k], key=lambda t: t[0])], 0) for k in range(mode_count)],
        0,
    )
    doubled = jnp.concatenate([stacked, stacked], 0)
    pivot_mine = lax.dynamic_slice_in_dim(doubled, (mode_count - mode_index) % mode_count * chunk, block, 0)

    swap = [(0, 1), (1, 0), (2, 3), (3, 2)]
    right_swap = [(2, 3), (3, 2)]
    other = lax.ppermute(panel_own, "col", swap)
    first_a = lax.ppermute(panel_own, "col", [(0, 2), (1, 3)])
    first_b = lax.ppermute(first_a, "col", right_swap)
    pivot_other = lax.ppermute(pivot_mine, "col", right_swap)

    s_mine = half * width
    s_other = width - s_mine
    out_cols = half * width

    def rows_of(mat, start):
        return lax.dynamic_slice_in_dim(mat, start, width, 0)

    inverse = jnp.where(col_index < 2, inverse_first, inverse_second)
    inv = lax.dynamic_slice_in_dim(inverse, out_cols, width, 1)
    direct = mm(panel_own, rows_of(inv, s_mine)) + mm(other, rows_of(inv, s_other))

    def left_side():
        return direct

    def right_side():
        q = mm(pivot_mine, rows_of(inv, s_mine)) + mm(pivot_other, rows_of(inv, s_other))
        z = mm(inverse_first, q)
        correction = mm(first_a, rows_of(z, s_mine)) + mm(first_b, rows_of(z, s_other))
        return direct - correction

    return lax.cond(col_index < 2, left_side, right_side)


def solution(mesh):
    return jax.shard_map(
        on_device,
        mesh=mesh,
        in_specs=(P(), P(), P(None, "mode", "col"), P(), P(), P(), P()),
        out_specs=P(("mode", "row"), "col"),
        check_vma=False,
    )
```

```python
import jax
import jax.numpy as jnp
from jax import lax
from jax.sharding import PartitionSpec as P

QMAX = 8


screen_rate = 6.0
bloch_phase = 0.7
real_amplitude = 0.15
identity_weight = 0.5

HIGHEST = lax.Precision.HIGHEST


def real_part(xr, yr, xc, yc):
    dx = xr[:, None] - xc[None, :]
    dy = yr[:, None] - yc[None, :]
    total = jnp.zeros(dx.shape, jnp.float32)
    for shift in (-1, 0, 1):
        total = total + jnp.cos(jnp.float32(bloch_phase * shift)) * jnp.exp(
            -screen_rate * ((dx - shift) ** 2 + dy * dy)
        )
    return total


def spectral_rows(xr, yr, wave, factor):
    theta = xr[:, None] * wave[0][None, :] + yr[:, None] * wave[1][None, :]
    cos_part = jnp.cos(theta).astype(jnp.bfloat16)
    sin_part = (-jnp.sin(theta)).astype(jnp.bfloat16)
    cos_part, sin_part = lax.optimization_barrier((cos_part, sin_part))
    spec = jnp.dot(cos_part, factor[0], preferred_element_type=jnp.float32)
    return spec + jnp.dot(sin_part, factor[1], preferred_element_type=jnp.float32)


def panel_rows(start, count, scale, coords, wave, factor, xc, yc, points):
    rows = start + jnp.arange(count, dtype=jnp.int32)
    xr = lax.dynamic_slice_in_dim(coords[0], start, count, 0)
    yr = lax.dynamic_slice_in_dim(coords[1], start, count, 0)
    spectral = spectral_rows(xr, yr, wave, factor)
    tile = real_amplitude * scale * real_part(xr, yr, xc, yc)
    diag = jnp.where(
        rows[:, None] == points[None, :], jnp.float32(identity_weight), jnp.float32(0.0)
    )
    return spectral + tile + diag


def mm(a, b):
    return jnp.dot(a, b, precision=HIGHEST, preferred_element_type=jnp.float32)


def on_device(coords, wave, col_factor, counts, blocks, inverse_first, inverse_second):
    row_count = lax.axis_size("row")
    mode_index = lax.axis_index("mode")
    row_index = lax.axis_index("row")
    col_index = lax.axis_index("col")
    block = inverse_first.shape[0]
    width = col_factor.shape[2]
    rows_dev = coords.shape[1] // (lax.axis_size("mode") * row_count)
    assert rows_dev == block and 2 * width == block
    group = mode_index * row_count + row_index

    factor = lax.all_gather(col_factor, "mode", axis=1, tiled=True)

    half = col_index % 2
    col_start = jnp.take(blocks, col_index // 2) * block + half * width
    points = col_start + jnp.arange(width, dtype=jnp.int32)
    xc = lax.dynamic_slice_in_dim(coords[0], col_start, width, 0)
    yc = lax.dynamic_slice_in_dim(coords[1], col_start, width, 0)

    own_start = group * rows_dev
    own_scale = jnp.take(counts, group).astype(jnp.float32) / QMAX
    panel_own = panel_rows(own_start, rows_dev, own_scale, coords, wave, factor, xc, yc, points)

    pivot_block = blocks[0]
    pivot_scale = jnp.take(counts, pivot_block).astype(jnp.float32) / QMAX
    pivot_mine = panel_rows(pivot_block * block, block, pivot_scale, coords, wave, factor, xc, yc, points)

    swap = [(0, 1), (1, 0), (2, 3), (3, 2)]
    right_swap = [(2, 3), (3, 2)]
    other = lax.ppermute(panel_own, "col", swap)
    pivot_other = lax.ppermute(pivot_mine, "col", right_swap)
    first_a = lax.ppermute(panel_own, "col", [(0, 2), (1, 3)])
    first_b = lax.ppermute(first_a, "col", right_swap)

    s_mine = half * width
    s_other = width - s_mine
    out_cols = half * width

    def rows_of(mat, start):
        return lax.dynamic_slice_in_dim(mat, start, width, 0)

    def left_side():
        inv = lax.dynamic_slice_in_dim(inverse_first, out_cols, width, 1)
        return mm(panel_own, rows_of(inv, s_mine)) + mm(other, rows_of(inv, s_other))

    def right_side():
        inv = lax.dynamic_slice_in_dim(inverse_second, out_cols, width, 1)
        q = mm(pivot_mine, rows_of(inv, s_mine)) + mm(pivot_other, rows_of(inv, s_other))
        z = mm(inverse_first, q)
        direct = mm(panel_own, rows_of(inv, s_mine)) + mm(other, rows_of(inv, s_other))
        correction = mm(first_a, rows_of(z, s_mine)) + mm(first_b, rows_of(z, s_other))
        return direct - correction

    return lax.cond(col_index < 2, left_side, right_side)


def solution(mesh):
    return jax.shard_map(
        on_device,
        mesh=mesh,
        in_specs=(P(), P(), P(None, "mode", "col"), P(), P(), P(), P()),
        out_specs=P(("mode", "row"), "col"),
        check_vma=False,
    )
```

```python
import jax
import jax.numpy as jnp
from jax import lax
from jax.sharding import PartitionSpec as P

QMAX = 8


screen_rate = 6.0
bloch_phase = 0.7
real_amplitude = 0.15
identity_weight = 0.5

HIGHEST = lax.Precision.HIGHEST


def real_part(xr, yr, xc, yc):
    dx = xr[:, None] - xc[None, :]
    dy = yr[:, None] - yc[None, :]
    total = jnp.zeros(dx.shape, jnp.float32)
    for shift in (-1, 0, 1):
        total = total + jnp.cos(jnp.float32(bloch_phase * shift)) * jnp.exp(
            -screen_rate * ((dx - shift) ** 2 + dy * dy)
        )
    return total


HALF_PI_PARTS = (1.5703125, 4.837512969970703125e-4, 7.54978995489188216e-8)
TWO_OVER_PI = 0.6366197723675814
SIN_COEFFS = (-1.9515295891e-4, 8.3321608736e-3, -1.6666654611e-1)
COS_COEFFS = (2.443315711809948e-5, -1.388731625493765e-3, 4.166664568298827e-2)


def cos_and_negsin(theta):
    f32 = jnp.float32
    k = jnp.round(theta * f32(TWO_OVER_PI))
    r = theta
    for part in HALF_PI_PARTS:
        r = r - k * f32(part)
    z = r * r
    s = ((f32(SIN_COEFFS[0]) * z + f32(SIN_COEFFS[1])) * z + f32(SIN_COEFFS[2])) * z * r + r
    c = ((f32(COS_COEFFS[0]) * z + f32(COS_COEFFS[1])) * z + f32(COS_COEFFS[2])) * z * z
    c = c - f32(0.5) * z + f32(1.0)
    quadrant = k - f32(4.0) * jnp.floor(k * f32(0.25))
    odd = (quadrant == 1.0) | (quadrant == 3.0)
    sin_r = jnp.where(odd, c, s)
    cos_r = jnp.where(odd, s, c)
    cos_theta = jnp.where((quadrant == 1.0) | (quadrant == 2.0), -cos_r, cos_r)
    negsin_theta = jnp.where(quadrant >= 2.0, sin_r, -sin_r)
    return cos_theta, negsin_theta


def spectral_rows(xr, yr, wave, factor):
    theta = xr[:, None] * wave[0][None, :] + yr[:, None] * wave[1][None, :]
    cos_theta, negsin_theta = cos_and_negsin(theta)
    cos_part = cos_theta.astype(jnp.bfloat16)
    sin_part = negsin_theta.astype(jnp.bfloat16)
    cos_part, sin_part = lax.optimization_barrier((cos_part, sin_part))
    spec = jnp.dot(cos_part, factor[0], preferred_element_type=jnp.float32)
    return spec + jnp.dot(sin_part, factor[1], preferred_element_type=jnp.float32)


def panel_rows(start, count, scale, coords, wave, factor, xc, yc, points):
    rows = start + jnp.arange(count, dtype=jnp.int32)
    xr = lax.dynamic_slice_in_dim(coords[0], start, count, 0)
    yr = lax.dynamic_slice_in_dim(coords[1], start, count, 0)
    spectral = spectral_rows(xr, yr, wave, factor)
    tile = real_amplitude * scale * real_part(xr, yr, xc, yc)
    diag = jnp.where(
        rows[:, None] == points[None, :], jnp.float32(identity_weight), jnp.float32(0.0)
    )
    return spectral + tile + diag


def mm(a, b):
    return jnp.dot(a, b, precision=HIGHEST, preferred_element_type=jnp.float32)


def on_device(coords, wave, col_factor, counts, blocks, inverse_first, inverse_second):
    row_count = lax.axis_size("row")
    mode_index = lax.axis_index("mode")
    row_index = lax.axis_index("row")
    col_index = lax.axis_index("col")
    block = inverse_first.shape[0]
    width = col_factor.shape[2]
    rows_dev = coords.shape[1] // (lax.axis_size("mode") * row_count)
    assert rows_dev == block and 2 * width == block
    group = mode_index * row_count + row_index

    factor = lax.all_gather(col_factor, "mode", axis=1, tiled=True)

    half = col_index % 2
    col_start = jnp.take(blocks, col_index // 2) * block + half * width
    points = col_start + jnp.arange(width, dtype=jnp.int32)
    xc = lax.dynamic_slice_in_dim(coords[0], col_start, width, 0)
    yc = lax.dynamic_slice_in_dim(coords[1], col_start, width, 0)

    own_start = group * rows_dev
    own_scale = jnp.take(counts, group).astype(jnp.float32) / QMAX
    panel_own = panel_rows(own_start, rows_dev, own_scale, coords, wave, factor, xc, yc, points)

    pivot_block = blocks[0]
    pivot_scale = jnp.take(counts, pivot_block).astype(jnp.float32) / QMAX
    pivot_mine = panel_rows(pivot_block * block, block, pivot_scale, coords, wave, factor, xc, yc, points)

    swap = [(0, 1), (1, 0), (2, 3), (3, 2)]
    right_swap = [(2, 3), (3, 2)]
    other = lax.ppermute(panel_own, "col", swap)
    pivot_other = lax.ppermute(pivot_mine, "col", right_swap)
    first_a = lax.ppermute(panel_own, "col", [(0, 2), (1, 3)])
    first_b = lax.ppermute(first_a, "col", right_swap)

    s_mine = half * width
    s_other = width - s_mine
    out_cols = half * width

    def rows_of(mat, start):
        return lax.dynamic_slice_in_dim(mat, start, width, 0)

    def left_side():
        inv = lax.dynamic_slice_in_dim(inverse_first, out_cols, width, 1)
        return mm(panel_own, rows_of(inv, s_mine)) + mm(other, rows_of(inv, s_other))

    def right_side():
        inv = lax.dynamic_slice_in_dim(inverse_second, out_cols, width, 1)
        q = mm(pivot_mine, rows_of(inv, s_mine)) + mm(pivot_other, rows_of(inv, s_other))
        z = mm(inverse_first, q)
        direct = mm(panel_own, rows_of(inv, s_mine)) + mm(other, rows_of(inv, s_other))
        correction = mm(first_a, rows_of(z, s_mine)) + mm(first_b, rows_of(z, s_other))
        return direct - correction

    return lax.cond(col_index < 2, left_side, right_side)


def solution(mesh):
    return jax.shard_map(
        on_device,
        mesh=mesh,
        in_specs=(P(), P(), P(None, "mode", "col"), P(), P(), P(), P()),
        out_specs=P(("mode", "row"), "col"),
        check_vma=False,
    )
```

```python
import jax
import jax.numpy as jnp
from jax import lax
from jax.sharding import PartitionSpec as P

QMAX = 8


screen_rate = 6.0
bloch_phase = 0.7
real_amplitude = 0.15
identity_weight = 0.5

HIGHEST = lax.Precision.HIGHEST


def real_part(xr, yr, xc, yc):
    dx = xr[:, None] - xc[None, :]
    dy = yr[:, None] - yc[None, :]
    total = jnp.zeros(dx.shape, jnp.float32)
    for shift in (-1, 0, 1):
        total = total + jnp.cos(jnp.float32(bloch_phase * shift)) * jnp.exp(
            -screen_rate * ((dx - shift) ** 2 + dy * dy)
        )
    return total


HALF_PI_PARTS = (1.5703125, 4.837512969970703125e-4, 7.54978995489188216e-8)
TWO_OVER_PI = 0.6366197723675814
SIN_COEFFS = (-1.9515295891e-4, 8.3321608736e-3, -1.6666654611e-1)
COS_COEFFS = (2.443315711809948e-5, -1.388731625493765e-3, 4.166664568298827e-2)


def cos_and_negsin(theta):
    f32 = jnp.float32
    k = jnp.round(theta * f32(TWO_OVER_PI))
    r = theta
    for part in HALF_PI_PARTS:
        r = r - k * f32(part)
    z = r * r
    s = ((f32(SIN_COEFFS[0]) * z + f32(SIN_COEFFS[1])) * z + f32(SIN_COEFFS[2])) * z * r + r
    c = ((f32(COS_COEFFS[0]) * z + f32(COS_COEFFS[1])) * z + f32(COS_COEFFS[2])) * z * z
    c = c - f32(0.5) * z + f32(1.0)
    quadrant = k - f32(4.0) * jnp.floor(k * f32(0.25))
    odd = (quadrant == 1.0) | (quadrant == 3.0)
    sin_r = jnp.where(odd, c, s)
    cos_r = jnp.where(odd, s, c)
    cos_theta = jnp.where((quadrant == 1.0) | (quadrant == 2.0), -cos_r, cos_r)
    negsin_theta = jnp.where(quadrant >= 2.0, sin_r, -sin_r)
    return cos_theta, negsin_theta


def spectral_rows(xr, yr, wave, factor):
    theta = xr[:, None] * wave[0][None, :] + yr[:, None] * wave[1][None, :]
    cos_theta, negsin_theta = cos_and_negsin(theta)
    cos_part = cos_theta.astype(jnp.bfloat16)
    sin_part = negsin_theta.astype(jnp.bfloat16)
    cos_part, sin_part = lax.optimization_barrier((cos_part, sin_part))
    spec = jnp.dot(cos_part, factor[0], preferred_element_type=jnp.float32)
    return spec + jnp.dot(sin_part, factor[1], preferred_element_type=jnp.float32)


def panel_rows(start, count, scale, coords, wave, factor, xc, yc, points):
    rows = start + jnp.arange(count, dtype=jnp.int32)
    xr = lax.dynamic_slice_in_dim(coords[0], start, count, 0)
    yr = lax.dynamic_slice_in_dim(coords[1], start, count, 0)
    spectral = spectral_rows(xr, yr, wave, factor)
    tile = real_amplitude * scale * real_part(xr, yr, xc, yc)
    diag = jnp.where(
        rows[:, None] == points[None, :], jnp.float32(identity_weight), jnp.float32(0.0)
    )
    return spectral + tile + diag


def mm(a, b):
    return jnp.dot(a, b, precision=HIGHEST, preferred_element_type=jnp.float32)


def on_device(coords, wave, col_factor, counts, blocks, inverse_first, inverse_second):
    row_count = lax.axis_size("row")
    mode_index = lax.axis_index("mode")
    row_index = lax.axis_index("row")
    col_index = lax.axis_index("col")
    block = inverse_first.shape[0]
    width = col_factor.shape[2]
    rows_dev = coords.shape[1] // (lax.axis_size("mode") * row_count)
    assert rows_dev == block and 2 * width == block
    group = mode_index * row_count + row_index

    factor = lax.all_gather(col_factor, "mode", axis=1, tiled=True)

    half = col_index % 2
    col_start = jnp.take(blocks, col_index // 2) * block + half * width
    points = col_start + jnp.arange(width, dtype=jnp.int32)
    xc = lax.dynamic_slice_in_dim(coords[0], col_start, width, 0)
    yc = lax.dynamic_slice_in_dim(coords[1], col_start, width, 0)

    own_start = group * rows_dev
    own_scale = jnp.take(counts, group).astype(jnp.float32) / QMAX
    panel_own = panel_rows(own_start, rows_dev, own_scale, coords, wave, factor, xc, yc, points)

    pivot_block = blocks[0]
    pivot_scale = jnp.take(counts, pivot_block).astype(jnp.float32) / QMAX
    pivot_mine = panel_rows(pivot_block * block, block, pivot_scale, coords, wave, factor, xc, yc, points)

    swap = [(0, 1), (1, 0), (2, 3), (3, 2)]
    right_swap = [(2, 3), (3, 2)]
    other = lax.ppermute(panel_own, "col", swap)
    pivot_other = lax.ppermute(pivot_mine, "col", right_swap)
    first_a = lax.ppermute(panel_own, "col", [(0, 2), (1, 3)])
    first_b = lax.ppermute(first_a, "col", right_swap)

    s_mine = half * width
    s_other = width - s_mine
    out_cols = half * width

    def rows_of(mat, start):
        return lax.dynamic_slice_in_dim(mat, start, width, 0)

    inverse = jnp.where(col_index < 2, inverse_first, inverse_second)
    inv = lax.dynamic_slice_in_dim(inverse, out_cols, width, 1)
    direct = mm(panel_own, rows_of(inv, s_mine)) + mm(other, rows_of(inv, s_other))
    q = mm(pivot_mine, rows_of(inv, s_mine)) + mm(pivot_other, rows_of(inv, s_other))
    z = mm(inverse_first, q)

    def left_side():
        return direct

    def right_side():
        correction = mm(first_a, rows_of(z, s_mine)) + mm(first_b, rows_of(z, s_other))
        return direct - correction

    return lax.cond(col_index < 2, left_side, right_side)


def solution(mesh):
    return jax.shard_map(
        on_device,
        mesh=mesh,
        in_specs=(P(), P(), P(None, "mode", "col"), P(), P(), P(), P()),
        out_specs=P(("mode", "row"), "col"),
        check_vma=False,
    )
```

```python
import jax
import jax.numpy as jnp
from jax import lax
from jax.sharding import PartitionSpec as P

QMAX = 8


screen_rate = 6.0
bloch_phase = 0.7
real_amplitude = 0.15
identity_weight = 0.5

HIGHEST = lax.Precision.HIGHEST


def real_part(xr, yr, xc, yc):
    dx = xr[:, None] - xc[None, :]
    dy = yr[:, None] - yc[None, :]
    total = jnp.zeros(dx.shape, jnp.float32)
    for shift in (-1, 0, 1):
        total = total + jnp.cos(jnp.float32(bloch_phase * shift)) * jnp.exp(
            -screen_rate * ((dx - shift) ** 2 + dy * dy)
        )
    return total


HALF_PI_PARTS = (1.5703125, 4.837512969970703125e-4, 7.54978995489188216e-8)
TWO_OVER_PI = 0.6366197723675814
SIN_COEFFS = (-1.9515295891e-4, 8.3321608736e-3, -1.6666654611e-1)
COS_COEFFS = (2.443315711809948e-5, -1.388731625493765e-3, 4.166664568298827e-2)


def cos_and_negsin(theta):
    f32 = jnp.float32
    k = jnp.round(theta * f32(TWO_OVER_PI))
    r = theta
    for part in HALF_PI_PARTS:
        r = r - k * f32(part)
    z = r * r
    s = ((f32(SIN_COEFFS[0]) * z + f32(SIN_COEFFS[1])) * z + f32(SIN_COEFFS[2])) * z * r + r
    c = ((f32(COS_COEFFS[0]) * z + f32(COS_COEFFS[1])) * z + f32(COS_COEFFS[2])) * z * z
    c = c - f32(0.5) * z + f32(1.0)
    quadrant = k - f32(4.0) * jnp.floor(k * f32(0.25))
    odd = (quadrant == 1.0) | (quadrant == 3.0)
    sin_r = jnp.where(odd, c, s)
    cos_r = jnp.where(odd, s, c)
    cos_theta = jnp.where((quadrant == 1.0) | (quadrant == 2.0), -cos_r, cos_r)
    negsin_theta = jnp.where(quadrant >= 2.0, sin_r, -sin_r)
    return cos_theta, negsin_theta


def spectral_rows(xr, yr, waves_of, factors):
    total = None
    for kvec, factor in zip(waves_of, factors):
        part = spectral_part(xr, yr, kvec, factor)
        total = part if total is None else total + part
    return total


def spectral_part(xr, yr, wave, factor):
    theta = xr[:, None] * wave[0][None, :] + yr[:, None] * wave[1][None, :]
    cos_theta, negsin_theta = cos_and_negsin(theta)
    cos_part = cos_theta.astype(jnp.bfloat16)
    sin_part = negsin_theta.astype(jnp.bfloat16)
    cos_part, sin_part = lax.optimization_barrier((cos_part, sin_part))
    spec = jnp.dot(cos_part, factor[0], preferred_element_type=jnp.float32)
    return spec + jnp.dot(sin_part, factor[1], preferred_element_type=jnp.float32)


def panel_rows(start, count, scale, coords, waves_of, factors, xc, yc, points):
    rows = start + jnp.arange(count, dtype=jnp.int32)
    xr = lax.dynamic_slice_in_dim(coords[0], start, count, 0)
    yr = lax.dynamic_slice_in_dim(coords[1], start, count, 0)
    spectral = spectral_rows(xr, yr, waves_of, factors)
    tile = real_amplitude * scale * real_part(xr, yr, xc, yc)
    diag = jnp.where(
        rows[:, None] == points[None, :], jnp.float32(identity_weight), jnp.float32(0.0)
    )
    return spectral + tile + diag


def mm(a, b):
    return jnp.dot(a, b, precision=HIGHEST, preferred_element_type=jnp.float32)


def on_device(coords, wave, col_factor, counts, blocks, inverse_first, inverse_second):
    row_count = lax.axis_size("row")
    mode_index = lax.axis_index("mode")
    row_index = lax.axis_index("row")
    col_index = lax.axis_index("col")
    block = inverse_first.shape[0]
    width = col_factor.shape[2]
    rows_dev = coords.shape[1] // (lax.axis_size("mode") * row_count)
    assert rows_dev == block and 2 * width == block
    group = mode_index * row_count + row_index

    local_modes = col_factor.shape[1]
    piece = local_modes // 2
    factors = [
        lax.all_gather(col_factor[:, h * piece:(h + 1) * piece, :], "mode", axis=1, tiled=True)
        for h in range(2)
    ]
    slices = wave.reshape(2, -1, local_modes)
    waves_of = [slices[:, :, h * piece:(h + 1) * piece].reshape(2, -1) for h in range(2)]

    half = col_index % 2
    col_start = jnp.take(blocks, col_index // 2) * block + half * width
    points = col_start + jnp.arange(width, dtype=jnp.int32)
    xc = lax.dynamic_slice_in_dim(coords[0], col_start, width, 0)
    yc = lax.dynamic_slice_in_dim(coords[1], col_start, width, 0)

    own_start = group * rows_dev
    own_scale = jnp.take(counts, group).astype(jnp.float32) / QMAX
    panel_own = panel_rows(own_start, rows_dev, own_scale, coords, waves_of, factors, xc, yc, points)

    pivot_block = blocks[0]
    pivot_scale = jnp.take(counts, pivot_block).astype(jnp.float32) / QMAX
    pivot_mine = panel_rows(pivot_block * block, block, pivot_scale, coords, waves_of, factors, xc, yc, points)

    swap = [(0, 1), (1, 0), (2, 3), (3, 2)]
    right_swap = [(2, 3), (3, 2)]
    other = lax.ppermute(panel_own, "col", swap)
    pivot_other = lax.ppermute(pivot_mine, "col", right_swap)
    first_a = lax.ppermute(panel_own, "col", [(0, 2), (1, 3)])
    first_b = lax.ppermute(first_a, "col", right_swap)

    s_mine = half * width
    s_other = width - s_mine
    out_cols = half * width

    def rows_of(mat, start):
        return lax.dynamic_slice_in_dim(mat, start, width, 0)

    inverse = jnp.where(col_index < 2, inverse_first, inverse_second)
    inv = lax.dynamic_slice_in_dim(inverse, out_cols, width, 1)
    direct = mm(panel_own, rows_of(inv, s_mine)) + mm(other, rows_of(inv, s_other))
    q = mm(pivot_mine, rows_of(inv, s_mine)) + mm(pivot_other, rows_of(inv, s_other))
    z = mm(inverse_first, q)

    correction = mm(first_a, rows_of(z, s_mine)) + mm(first_b, rows_of(z, s_other))
    return direct - correction


def solution(mesh):
    return jax.shard_map(
        on_device,
        mesh=mesh,
        in_specs=(P(), P(), P(None, "mode", "col"), P(), P(), P(), P()),
        out_specs=P(("mode", "row"), "col"),
        check_vma=False,
    )
```

```python
import jax
import jax.numpy as jnp
from jax import lax
from jax.sharding import PartitionSpec as P

QMAX = 8


screen_rate = 6.0
bloch_phase = 0.7
real_amplitude = 0.15
identity_weight = 0.5

HIGHEST = lax.Precision.HIGHEST


def real_part(xr, yr, xc, yc):
    dx = xr[:, None] - xc[None, :]
    dy = yr[:, None] - yc[None, :]
    total = jnp.zeros(dx.shape, jnp.float32)
    for shift in (-1, 0, 1):
        total = total + jnp.cos(jnp.float32(bloch_phase * shift)) * jnp.exp(
            -screen_rate * ((dx - shift) ** 2 + dy * dy)
        )
    return total


HALF_PI_PARTS = (1.5703125, 4.837512969970703125e-4, 7.54978995489188216e-8)
TWO_OVER_PI = 0.6366197723675814
SIN_COEFFS = (-1.9515295891e-4, 8.3321608736e-3, -1.6666654611e-1)
COS_COEFFS = (2.443315711809948e-5, -1.388731625493765e-3, 4.166664568298827e-2)


def cos_and_negsin(theta):
    f32 = jnp.float32
    k = jnp.round(theta * f32(TWO_OVER_PI))
    r = theta
    for part in HALF_PI_PARTS:
        r = r - k * f32(part)
    z = r * r
    s = ((f32(SIN_COEFFS[0]) * z + f32(SIN_COEFFS[1])) * z + f32(SIN_COEFFS[2])) * z * r + r
    c = ((f32(COS_COEFFS[0]) * z + f32(COS_COEFFS[1])) * z + f32(COS_COEFFS[2])) * z * z
    c = c - f32(0.5) * z + f32(1.0)
    quadrant = k - f32(4.0) * jnp.floor(k * f32(0.25))
    odd = (quadrant == 1.0) | (quadrant == 3.0)
    sin_r = jnp.where(odd, c, s)
    cos_r = jnp.where(odd, s, c)
    cos_theta = jnp.where((quadrant == 1.0) | (quadrant == 2.0), -cos_r, cos_r)
    negsin_theta = jnp.where(quadrant >= 2.0, sin_r, -sin_r)
    return cos_theta, negsin_theta


def make_waves(xr, yr, kvec):
    theta = xr[:, None] * kvec[0][None, :] + yr[:, None] * kvec[1][None, :]
    cos_theta, negsin_theta = cos_and_negsin(theta)
    return lax.optimization_barrier((cos_theta.astype(jnp.bfloat16), negsin_theta.astype(jnp.bfloat16)))


def wave_product(waves, factor):
    cos_part, sin_part = waves
    spec = jnp.dot(cos_part, factor[0], preferred_element_type=jnp.float32)
    return spec + jnp.dot(sin_part, factor[1], preferred_element_type=jnp.float32)


def ring_gather(x, axis, n, split_axis):
    fwd = [(i, (i + 1) % n) for i in range(n)]
    bwd = [(i, (i - 1) % n) for i in range(n)]
    pieces = [(0, x, None)]
    ahead, behind = x, x
    far = n // 2
    for step in range(1, far + 1):
        if step < far or n % 2 == 1:
            behind = lax.ppermute(behind, axis, fwd)
            ahead = lax.ppermute(ahead, axis, bwd)
            pieces.append((-step, behind, None))
            pieces.append((step, ahead, None))
        else:
            size = x.shape[split_axis] // 2
            lo = lax.slice_in_dim(behind, 0, size, axis=split_axis)
            hi = lax.slice_in_dim(ahead, size, 2 * size, axis=split_axis)
            pieces.append((step, lax.ppermute(lo, axis, fwd), 0))
            pieces.append((step, lax.ppermute(hi, axis, bwd), 1))
    return pieces


def mm(a, b):
    return jnp.dot(a, b, precision=HIGHEST, preferred_element_type=jnp.float32)


def on_device(coords, wave, col_factor, counts, blocks, inverse_first, inverse_second):
    mode_count = lax.axis_size("mode")
    row_count = lax.axis_size("row")
    mode_index = lax.axis_index("mode")
    row_index = lax.axis_index("row")
    col_index = lax.axis_index("col")
    block = inverse_first.shape[0]
    width = col_factor.shape[2]
    local_modes = col_factor.shape[1]
    rows_dev = coords.shape[1] // (mode_count * row_count)
    assert rows_dev == block and 2 * width == block
    group = mode_index * row_count + row_index

    half = col_index % 2
    col_start = jnp.take(blocks, col_index // 2) * block + half * width
    points = col_start + jnp.arange(width, dtype=jnp.int32)
    xc = lax.dynamic_slice_in_dim(coords[0], col_start, width, 0)
    yc = lax.dynamic_slice_in_dim(coords[1], col_start, width, 0)

    own_start = group * rows_dev
    xr = lax.dynamic_slice_in_dim(coords[0], own_start, rows_dev, 0)
    yr = lax.dynamic_slice_in_dim(coords[1], own_start, rows_dev, 0)
    pivot_block = blocks[0]
    pivot_start = pivot_block * block
    xp = lax.dynamic_slice_in_dim(coords[0], pivot_start, block, 0)
    yp = lax.dynamic_slice_in_dim(coords[1], pivot_start, block, 0)

    spectral = jnp.zeros((rows_dev, width), jnp.float32)
    pivot_spectral = jnp.zeros((block, width), jnp.float32)
    for offset, piece, part in ring_gather(col_factor, "mode", mode_count, 1):
        source = (mode_index + offset) % mode_count
        count = piece.shape[1]
        first_mode = source * local_modes + (0 if part is None else part * count)
        piece, xr_s, yr_s, xp_s, yp_s = lax.optimization_barrier((piece, xr, yr, xp, yp))
        kvec = lax.dynamic_slice_in_dim(wave, first_mode, count, 1)
        spectral = spectral + wave_product(make_waves(xr_s, yr_s, kvec), piece)
        pivot_spectral = pivot_spectral + wave_product(make_waves(xp_s, yp_s, kvec), piece)

    own_rows = own_start + jnp.arange(rows_dev, dtype=jnp.int32)
    own_scale = jnp.take(counts, group).astype(jnp.float32) / QMAX
    panel_own = (
        spectral
        + real_amplitude * own_scale * real_part(xr, yr, xc, yc)
        + jnp.where(own_rows[:, None] == points[None, :], jnp.float32(identity_weight), jnp.float32(0.0))
    )
    pivot_rows = pivot_start + jnp.arange(block, dtype=jnp.int32)
    pivot_scale = jnp.take(counts, pivot_block).astype(jnp.float32) / QMAX
    pivot_mine = (
        pivot_spectral
        + real_amplitude * pivot_scale * real_part(xp, yp, xc, yc)
        + jnp.where(pivot_rows[:, None] == points[None, :], jnp.float32(identity_weight), jnp.float32(0.0))
    )

    swap = [(0, 1), (1, 0), (2, 3), (3, 2)]
    right_swap = [(2, 3), (3, 2)]
    other = lax.ppermute(panel_own, "col", swap)
    pivot_other = lax.ppermute(pivot_mine, "col", right_swap)
    first_a = lax.ppermute(panel_own, "col", [(0, 2), (1, 3)])
    first_b = lax.ppermute(first_a, "col", right_swap)

    s_mine = half * width
    s_other = width - s_mine
    out_cols = half * width

    def rows_of(mat, start):
        return lax.dynamic_slice_in_dim(mat, start, width, 0)

    inverse = jnp.where(col_index < 2, inverse_first, inverse_second)
    inv = lax.dynamic_slice_in_dim(inverse, out_cols, width, 1)
    direct = mm(panel_own, rows_of(inv, s_mine)) + mm(other, rows_of(inv, s_other))
    q = mm(pivot_mine, rows_of(inv, s_mine)) + mm(pivot_other, rows_of(inv, s_other))
    z = mm(inverse_first, q)
    correction = mm(first_a, rows_of(z, s_mine)) + mm(first_b, rows_of(z, s_other))
    return direct - correction


def solution(mesh):
    return jax.shard_map(
        on_device,
        mesh=mesh,
        in_specs=(P(), P(), P(None, "mode", "col"), P(), P(), P(), P()),
        out_specs=P(("mode", "row"), "col"),
        check_vma=False,
    )
```

```python
import jax
import jax.numpy as jnp
from jax import lax
from jax.sharding import PartitionSpec as P

QMAX = 8


screen_rate = 6.0
bloch_phase = 0.7
real_amplitude = 0.15
identity_weight = 0.5

HIGHEST = lax.Precision.HIGHEST


def real_part(xr, yr, xc, yc):
    dx = xr[:, None] - xc[None, :]
    dy = yr[:, None] - yc[None, :]
    total = jnp.zeros(dx.shape, jnp.float32)
    for shift in (-1, 0, 1):
        total = total + jnp.cos(jnp.float32(bloch_phase * shift)) * jnp.exp(
            -screen_rate * ((dx - shift) ** 2 + dy * dy)
        )
    return total


HALF_PI_PARTS = (1.5703125, 4.837512969970703125e-4, 7.54978995489188216e-8)
TWO_OVER_PI = 0.6366197723675814
SIN_COEFFS = (-1.9515295891e-4, 8.3321608736e-3, -1.6666654611e-1)
COS_COEFFS = (2.443315711809948e-5, -1.388731625493765e-3, 4.166664568298827e-2)


def cos_and_negsin(theta):
    f32 = jnp.float32
    k = jnp.round(theta * f32(TWO_OVER_PI))
    r = theta
    for part in HALF_PI_PARTS:
        r = r - k * f32(part)
    z = r * r
    s = ((f32(SIN_COEFFS[0]) * z + f32(SIN_COEFFS[1])) * z + f32(SIN_COEFFS[2])) * z * r + r
    c = ((f32(COS_COEFFS[0]) * z + f32(COS_COEFFS[1])) * z + f32(COS_COEFFS[2])) * z * z
    c = c - f32(0.5) * z + f32(1.0)
    quadrant = k - f32(4.0) * jnp.floor(k * f32(0.25))
    odd = (quadrant == 1.0) | (quadrant == 3.0)
    sin_r = jnp.where(odd, c, s)
    cos_r = jnp.where(odd, s, c)
    cos_theta = jnp.where((quadrant == 1.0) | (quadrant == 2.0), -cos_r, cos_r)
    negsin_theta = jnp.where(quadrant >= 2.0, sin_r, -sin_r)
    return cos_theta, negsin_theta


def spectral_rows(xr, yr, wave, factor):
    theta = xr[:, None] * wave[0][None, :] + yr[:, None] * wave[1][None, :]
    cos_theta, negsin_theta = cos_and_negsin(theta)
    cos_part = cos_theta.astype(jnp.bfloat16)
    sin_part = negsin_theta.astype(jnp.bfloat16)
    cos_part, sin_part = lax.optimization_barrier((cos_part, sin_part))
    spec = jnp.dot(cos_part, factor[0], preferred_element_type=jnp.float32)
    return spec + jnp.dot(sin_part, factor[1], preferred_element_type=jnp.float32)


def panel_rows(start, count, scale, coords, wave, factor, xc, yc, points):
    rows = start + jnp.arange(count, dtype=jnp.int32)
    xr = lax.dynamic_slice_in_dim(coords[0], start, count, 0)
    yr = lax.dynamic_slice_in_dim(coords[1], start, count, 0)
    spectral = spectral_rows(xr, yr, wave, factor)
    tile = real_amplitude * scale * real_part(xr, yr, xc, yc)
    diag = jnp.where(
        rows[:, None] == points[None, :], jnp.float32(identity_weight), jnp.float32(0.0)
    )
    return spectral + tile + diag


def mm(a, b):
    return jnp.dot(a, b, precision=HIGHEST, preferred_element_type=jnp.float32)


def mm_high(a, b):
    return jnp.dot(a, b, precision=lax.Precision.HIGH, preferred_element_type=jnp.float32)


def on_device(coords, wave, col_factor, counts, blocks, inverse_first, inverse_second):
    row_count = lax.axis_size("row")
    mode_index = lax.axis_index("mode")
    row_index = lax.axis_index("row")
    col_index = lax.axis_index("col")
    block = inverse_first.shape[0]
    width = col_factor.shape[2]
    rows_dev = coords.shape[1] // (lax.axis_size("mode") * row_count)
    assert rows_dev == block and 2 * width == block
    group = mode_index * row_count + row_index

    factor = lax.all_gather(col_factor, "mode", axis=1, tiled=True)

    half = col_index % 2
    col_start = jnp.take(blocks, col_index // 2) * block + half * width
    points = col_start + jnp.arange(width, dtype=jnp.int32)
    xc = lax.dynamic_slice_in_dim(coords[0], col_start, width, 0)
    yc = lax.dynamic_slice_in_dim(coords[1], col_start, width, 0)

    own_start = group * rows_dev
    own_scale = jnp.take(counts, group).astype(jnp.float32) / QMAX
    panel_own = panel_rows(own_start, rows_dev, own_scale, coords, wave, factor, xc, yc, points)

    pivot_block = blocks[0]
    pivot_scale = jnp.take(counts, pivot_block).astype(jnp.float32) / QMAX
    pivot_mine = panel_rows(pivot_block * block, block, pivot_scale, coords, wave, factor, xc, yc, points)

    swap = [(0, 1), (1, 0), (2, 3), (3, 2)]
    right_swap = [(2, 3), (3, 2)]
    other = lax.ppermute(panel_own, "col", swap)
    pivot_other = lax.ppermute(pivot_mine, "col", right_swap)
    first_a = lax.ppermute(panel_own, "col", [(0, 2), (1, 3)])
    first_b = lax.ppermute(first_a, "col", right_swap)

    s_mine = half * width
    s_other = width - s_mine
    out_cols = half * width

    def rows_of(mat, start):
        return lax.dynamic_slice_in_dim(mat, start, width, 0)

    inverse = jnp.where(col_index < 2, inverse_first, inverse_second)
    inv = lax.dynamic_slice_in_dim(inverse, out_cols, width, 1)
    direct = mm(panel_own, rows_of(inv, s_mine)) + mm(other, rows_of(inv, s_other))
    q = mm(pivot_mine, rows_of(inv, s_mine)) + mm(pivot_other, rows_of(inv, s_other))
    z = mm(inverse_first, q)

    correction = mm_high(first_a, rows_of(z, s_mine)) + mm_high(first_b, rows_of(z, s_other))
    return direct - correction


def solution(mesh):
    return jax.shard_map(
        on_device,
        mesh=mesh,
        in_specs=(P(), P(), P(None, "mode", "col"), P(), P(), P(), P()),
        out_specs=P(("mode", "row"), "col"),
        check_vma=False,
    )
```

```python
import jax
import jax.numpy as jnp
from jax import lax
from jax.sharding import PartitionSpec as P

QMAX = 8


screen_rate = 6.0
bloch_phase = 0.7
real_amplitude = 0.15
identity_weight = 0.5

HIGHEST = lax.Precision.HIGHEST


def real_part(xr, yr, xc, yc):
    dx = xr[:, None] - xc[None, :]
    dy = yr[:, None] - yc[None, :]
    total = jnp.zeros(dx.shape, jnp.float32)
    for shift in (-1, 0, 1):
        total = total + jnp.cos(jnp.float32(bloch_phase * shift)) * jnp.exp(
            -screen_rate * ((dx - shift) ** 2 + dy * dy)
        )
    return total


HALF_PI_PARTS = (1.5703125, 4.837512969970703125e-4, 7.54978995489188216e-8)
TWO_OVER_PI = 0.6366197723675814
SIN_COEFFS = (-1.9515295891e-4, 8.3321608736e-3, -1.6666654611e-1)
COS_COEFFS = (2.443315711809948e-5, -1.388731625493765e-3, 4.166664568298827e-2)


def cos_and_negsin(theta):
    f32 = jnp.float32
    k = jnp.round(theta * f32(TWO_OVER_PI))
    r = theta
    for part in HALF_PI_PARTS:
        r = r - k * f32(part)
    z = r * r
    s = ((f32(SIN_COEFFS[0]) * z + f32(SIN_COEFFS[1])) * z + f32(SIN_COEFFS[2])) * z * r + r
    c = ((f32(COS_COEFFS[0]) * z + f32(COS_COEFFS[1])) * z + f32(COS_COEFFS[2])) * z * z
    c = c - f32(0.5) * z + f32(1.0)
    quadrant = k - f32(4.0) * jnp.floor(k * f32(0.25))
    odd = (quadrant == 1.0) | (quadrant == 3.0)
    sin_r = jnp.where(odd, c, s)
    cos_r = jnp.where(odd, s, c)
    cos_theta = jnp.where((quadrant == 1.0) | (quadrant == 2.0), -cos_r, cos_r)
    negsin_theta = jnp.where(quadrant >= 2.0, sin_r, -sin_r)
    return cos_theta, negsin_theta


def spectral_rows(xr, yr, wave, factor, pieces=1):
    theta = xr[:, None] * wave[0][None, :] + yr[:, None] * wave[1][None, :]
    cos_theta, negsin_theta = cos_and_negsin(theta)
    cos_part = cos_theta.astype(jnp.bfloat16)
    sin_part = negsin_theta.astype(jnp.bfloat16)
    cos_part, sin_part = lax.optimization_barrier((cos_part, sin_part))
    rows = cos_part.shape[0] // pieces
    out = []
    for p in range(pieces):
        spec = jnp.dot(cos_part[p * rows:(p + 1) * rows], factor[0], preferred_element_type=jnp.float32)
        out.append(spec + jnp.dot(sin_part[p * rows:(p + 1) * rows], factor[1], preferred_element_type=jnp.float32))
    return out if pieces > 1 else out[0]


def panel_rows(start, count, scale, coords, wave, factor, xc, yc, points, pieces=1):
    xr = lax.dynamic_slice_in_dim(coords[0], start, count, 0)
    yr = lax.dynamic_slice_in_dim(coords[1], start, count, 0)
    spectral = spectral_rows(xr, yr, wave, factor, pieces)
    if pieces == 1:
        spectral = [spectral]
    size = count // pieces
    out = []
    for p, spec in enumerate(spectral):
        rows = start + p * size + jnp.arange(size, dtype=jnp.int32)
        xs, ys = xr[p * size:(p + 1) * size], yr[p * size:(p + 1) * size]
        tile = real_amplitude * scale * real_part(xs, ys, xc, yc)
        diag = jnp.where(
            rows[:, None] == points[None, :], jnp.float32(identity_weight), jnp.float32(0.0)
        )
        out.append(spec + tile + diag)
    return out if pieces > 1 else out[0]


def mm(a, b):
    return jnp.dot(a, b, precision=HIGHEST, preferred_element_type=jnp.float32)


def mm_high(a, b):
    return jnp.dot(a, b, precision=lax.Precision.HIGH, preferred_element_type=jnp.float32)


def on_device(coords, wave, col_factor, counts, blocks, inverse_first, inverse_second):
    row_count = lax.axis_size("row")
    mode_index = lax.axis_index("mode")
    row_index = lax.axis_index("row")
    col_index = lax.axis_index("col")
    block = inverse_first.shape[0]
    width = col_factor.shape[2]
    rows_dev = coords.shape[1] // (lax.axis_size("mode") * row_count)
    assert rows_dev == block and 2 * width == block
    group = mode_index * row_count + row_index

    factor = lax.all_gather(col_factor, "mode", axis=1, tiled=True)

    half = col_index % 2
    col_start = jnp.take(blocks, col_index // 2) * block + half * width
    points = col_start + jnp.arange(width, dtype=jnp.int32)
    xc = lax.dynamic_slice_in_dim(coords[0], col_start, width, 0)
    yc = lax.dynamic_slice_in_dim(coords[1], col_start, width, 0)

    own_start = group * rows_dev
    own_scale = jnp.take(counts, group).astype(jnp.float32) / QMAX
    panel_parts = panel_rows(own_start, rows_dev, own_scale, coords, wave, factor, xc, yc, points, 2)
    panel_own = jnp.concatenate(panel_parts, 0)

    pivot_block = blocks[0]
    pivot_scale = jnp.take(counts, pivot_block).astype(jnp.float32) / QMAX
    pivot_mine = panel_rows(pivot_block * block, block, pivot_scale, coords, wave, factor, xc, yc, points)

    swap = [(0, 1), (1, 0), (2, 3), (3, 2)]
    right_swap = [(2, 3), (3, 2)]
    other = lax.ppermute(panel_own, "col", swap)
    pivot_other = lax.ppermute(pivot_mine, "col", right_swap)
    first_a = [lax.ppermute(part, "col", [(0, 2), (1, 3)]) for part in panel_parts]
    first_b = [lax.ppermute(part, "col", right_swap) for part in first_a]

    s_mine = half * width
    s_other = width - s_mine
    out_cols = half * width

    def rows_of(mat, start):
        return lax.dynamic_slice_in_dim(mat, start, width, 0)

    inverse = jnp.where(col_index < 2, inverse_first, inverse_second)
    inv = lax.dynamic_slice_in_dim(inverse, out_cols, width, 1)
    direct = mm(panel_own, rows_of(inv, s_mine)) + mm(other, rows_of(inv, s_other))
    q = mm(pivot_mine, rows_of(inv, s_mine)) + mm(pivot_other, rows_of(inv, s_other))
    z = mm(inverse_first, q)

    size = rows_dev // len(panel_parts)
    outs = []
    for p in range(len(panel_parts)):
        direct_p = direct[p * size:(p + 1) * size]

        def left_side(direct_p=direct_p):
            return direct_p

        def right_side(direct_p=direct_p, p=p):
            correction = mm_high(first_a[p], rows_of(z, s_mine)) + mm_high(first_b[p], rows_of(z, s_other))
            return direct_p - correction

        outs.append(lax.cond(col_index < 2, left_side, right_side))
    return jnp.concatenate(outs, 0)


def solution(mesh):
    return jax.shard_map(
        on_device,
        mesh=mesh,
        in_specs=(P(), P(), P(None, "mode", "col"), P(), P(), P(), P()),
        out_specs=P(("mode", "row"), "col"),
        check_vma=False,
    )
```

```python
import jax
import jax.numpy as jnp
from jax import lax
from jax.sharding import PartitionSpec as P

QMAX = 8


screen_rate = 6.0
bloch_phase = 0.7
real_amplitude = 0.15
identity_weight = 0.5

HIGHEST = lax.Precision.HIGHEST


def real_part(xr, yr, xc, yc):
    dx = xr[:, None] - xc[None, :]
    dy = yr[:, None] - yc[None, :]
    total = jnp.zeros(dx.shape, jnp.float32)
    for shift in (-1, 0, 1):
        total = total + jnp.cos(jnp.float32(bloch_phase * shift)) * jnp.exp(
            -screen_rate * ((dx - shift) ** 2 + dy * dy)
        )
    return total


HALF_PI_PARTS = (1.5703125, 4.837512969970703125e-4, 7.54978995489188216e-8)
TWO_OVER_PI = 0.6366197723675814
SIN_COEFFS = (-1.9515295891e-4, 8.3321608736e-3, -1.6666654611e-1)
COS_COEFFS = (2.443315711809948e-5, -1.388731625493765e-3, 4.166664568298827e-2)


def cos_and_negsin(theta):
    f32 = jnp.float32
    k = jnp.round(theta * f32(TWO_OVER_PI))
    r = theta
    for part in HALF_PI_PARTS:
        r = r - k * f32(part)
    z = r * r
    s = ((f32(SIN_COEFFS[0]) * z + f32(SIN_COEFFS[1])) * z + f32(SIN_COEFFS[2])) * z * r + r
    c = ((f32(COS_COEFFS[0]) * z + f32(COS_COEFFS[1])) * z + f32(COS_COEFFS[2])) * z * z
    c = c - f32(0.5) * z + f32(1.0)
    quadrant = k - f32(4.0) * jnp.floor(k * f32(0.25))
    odd = (quadrant == 1.0) | (quadrant == 3.0)
    sin_r = jnp.where(odd, c, s)
    cos_r = jnp.where(odd, s, c)
    cos_theta = jnp.where((quadrant == 1.0) | (quadrant == 2.0), -cos_r, cos_r)
    negsin_theta = jnp.where(quadrant >= 2.0, sin_r, -sin_r)
    return cos_theta, negsin_theta


def spectral_rows(xr, yr, wave, factor, pieces=1):
    theta = xr[:, None] * wave[0][None, :] + yr[:, None] * wave[1][None, :]
    cos_theta, negsin_theta = cos_and_negsin(theta)
    cos_part = cos_theta.astype(jnp.bfloat16)
    sin_part = negsin_theta.astype(jnp.bfloat16)
    cos_part, sin_part = lax.optimization_barrier((cos_part, sin_part))
    rows = cos_part.shape[0] // pieces
    out = []
    for p in range(pieces):
        spec = jnp.dot(cos_part[p * rows:(p + 1) * rows], factor[0], preferred_element_type=jnp.float32)
        out.append(spec + jnp.dot(sin_part[p * rows:(p + 1) * rows], factor[1], preferred_element_type=jnp.float32))
    return out if pieces > 1 else out[0]


def panel_rows(start, count, scale, coords, wave, factor, xc, yc, points, pieces=1):
    xr = lax.dynamic_slice_in_dim(coords[0], start, count, 0)
    yr = lax.dynamic_slice_in_dim(coords[1], start, count, 0)
    spectral = spectral_rows(xr, yr, wave, factor, pieces)
    if pieces == 1:
        spectral = [spectral]
    size = count // pieces
    out = []
    for p, spec in enumerate(spectral):
        rows = start + p * size + jnp.arange(size, dtype=jnp.int32)
        xs, ys = xr[p * size:(p + 1) * size], yr[p * size:(p + 1) * size]
        tile = real_amplitude * scale * real_part(xs, ys, xc, yc)
        diag = jnp.where(
            rows[:, None] == points[None, :], jnp.float32(identity_weight), jnp.float32(0.0)
        )
        tile, diag = lax.optimization_barrier((tile, diag))
        out.append(spec + tile + diag)
    return out if pieces > 1 else out[0]


def mm(a, b):
    return jnp.dot(a, b, precision=HIGHEST, preferred_element_type=jnp.float32)


def mm_high(a, b):
    return jnp.dot(a, b, precision=lax.Precision.HIGH, preferred_element_type=jnp.float32)


def on_device(coords, wave, col_factor, counts, blocks, inverse_first, inverse_second):
    row_count = lax.axis_size("row")
    mode_index = lax.axis_index("mode")
    row_index = lax.axis_index("row")
    col_index = lax.axis_index("col")
    block = inverse_first.shape[0]
    width = col_factor.shape[2]
    rows_dev = coords.shape[1] // (lax.axis_size("mode") * row_count)
    assert rows_dev == block and 2 * width == block
    group = mode_index * row_count + row_index

    factor = lax.all_gather(col_factor, "mode", axis=1, tiled=True)

    half = col_index % 2
    col_start = jnp.take(blocks, col_index // 2) * block + half * width
    points = col_start + jnp.arange(width, dtype=jnp.int32)
    xc = lax.dynamic_slice_in_dim(coords[0], col_start, width, 0)
    yc = lax.dynamic_slice_in_dim(coords[1], col_start, width, 0)

    own_start = group * rows_dev
    own_scale = jnp.take(counts, group).astype(jnp.float32) / QMAX
    panel_parts = panel_rows(own_start, rows_dev, own_scale, coords, wave, factor, xc, yc, points, 2)
    panel_own = jnp.concatenate(panel_parts, 0)

    pivot_block = blocks[0]
    pivot_scale = jnp.take(counts, pivot_block).astype(jnp.float32) / QMAX
    pivot_mine = panel_rows(pivot_block * block, block, pivot_scale, coords, wave, factor, xc, yc, points)

    swap = [(0, 1), (1, 0), (2, 3), (3, 2)]
    right_swap = [(2, 3), (3, 2)]
    other = lax.ppermute(panel_own, "col", swap)
    pivot_other = lax.ppermute(pivot_mine, "col", right_swap)
    first_a = [lax.ppermute(part, "col", [(0, 2), (1, 3)]) for part in panel_parts]
    first_b = [lax.ppermute(part, "col", right_swap) for part in first_a]

    s_mine = half * width
    s_other = width - s_mine
    out_cols = half * width

    def rows_of(mat, start):
        return lax.dynamic_slice_in_dim(mat, start, width, 0)

    inverse = jnp.where(col_index < 2, inverse_first, inverse_second)
    inv = lax.dynamic_slice_in_dim(inverse, out_cols, width, 1)
    direct = mm(panel_own, rows_of(inv, s_mine)) + mm(other, rows_of(inv, s_other))
    q = mm(pivot_mine, rows_of(inv, s_mine)) + mm(pivot_other, rows_of(inv, s_other))
    z = mm(inverse_first, q)

    size = rows_dev // len(panel_parts)
    outs = []
    for p in range(len(panel_parts)):
        direct_p = direct[p * size:(p + 1) * size]

        def left_side(direct_p=direct_p):
            return direct_p

        def right_side(direct_p=direct_p, p=p):
            correction = mm_high(first_a[p], rows_of(z, s_mine)) + mm_high(first_b[p], rows_of(z, s_other))
            return direct_p - correction

        outs.append(lax.cond(col_index < 2, left_side, right_side))
    return jnp.concatenate(outs, 0)


def solution(mesh):
    return jax.shard_map(
        on_device,
        mesh=mesh,
        in_specs=(P(), P(), P(None, "mode", "col"), P(), P(), P(), P()),
        out_specs=P(("mode", "row"), "col"),
        check_vma=False,
    )
```

```python
import jax
import jax.numpy as jnp
from jax import lax
from jax.sharding import PartitionSpec as P

QMAX = 8


screen_rate = 6.0
bloch_phase = 0.7
real_amplitude = 0.15
identity_weight = 0.5

HIGHEST = lax.Precision.HIGHEST


def real_part(xr, yr, xc, yc):
    dx = xr[:, None] - xc[None, :]
    dy = yr[:, None] - yc[None, :]
    total = jnp.zeros(dx.shape, jnp.float32)
    for shift in (-1, 0, 1):
        total = total + jnp.cos(jnp.float32(bloch_phase * shift)) * jnp.exp(
            -screen_rate * ((dx - shift) ** 2 + dy * dy)
        )
    return total


HALF_PI_PARTS = (1.5703125, 4.837512969970703125e-4, 7.54978995489188216e-8)
TWO_OVER_PI = 0.6366197723675814
SIN_COEFFS = (-1.9515295891e-4, 8.3321608736e-3, -1.6666654611e-1)
COS_COEFFS = (2.443315711809948e-5, -1.388731625493765e-3, 4.166664568298827e-2)


def cos_and_negsin(theta):
    f32 = jnp.float32
    k = jnp.round(theta * f32(TWO_OVER_PI))
    r = theta
    for part in HALF_PI_PARTS:
        r = r - k * f32(part)
    z = r * r
    s = ((f32(SIN_COEFFS[0]) * z + f32(SIN_COEFFS[1])) * z + f32(SIN_COEFFS[2])) * z * r + r
    c = ((f32(COS_COEFFS[0]) * z + f32(COS_COEFFS[1])) * z + f32(COS_COEFFS[2])) * z * z
    c = c - f32(0.5) * z + f32(1.0)
    quadrant = k - f32(4.0) * jnp.floor(k * f32(0.25))
    odd = (quadrant == 1.0) | (quadrant == 3.0)
    sin_r = jnp.where(odd, c, s)
    cos_r = jnp.where(odd, s, c)
    cos_theta = jnp.where((quadrant == 1.0) | (quadrant == 2.0), -cos_r, cos_r)
    negsin_theta = jnp.where(quadrant >= 2.0, sin_r, -sin_r)
    return cos_theta, negsin_theta


def make_waves(xr, yr, wave):
    theta = xr[:, None] * wave[0][None, :] + yr[:, None] * wave[1][None, :]
    cos_theta, negsin_theta = cos_and_negsin(theta)
    return lax.optimization_barrier((cos_theta.astype(jnp.bfloat16), negsin_theta.astype(jnp.bfloat16)))


def wave_product(waves, factor, start=0, rows=None):
    cos_part, sin_part = waves
    rows = cos_part.shape[0] if rows is None else rows
    spec = jnp.dot(cos_part[start:start + rows], factor[0], preferred_element_type=jnp.float32)
    return spec + jnp.dot(sin_part[start:start + rows], factor[1], preferred_element_type=jnp.float32)


def tile_and_diag(start, count, scale, xr, yr, xc, yc, points):
    rows = start + jnp.arange(count, dtype=jnp.int32)
    tile = real_amplitude * scale * real_part(xr, yr, xc, yc)
    diag = jnp.where(rows[:, None] == points[None, :], jnp.float32(identity_weight), jnp.float32(0.0))
    return lax.optimization_barrier((tile, diag))


def mm(a, b):
    return jnp.dot(a, b, precision=HIGHEST, preferred_element_type=jnp.float32)


def mm_high(a, b):
    return jnp.dot(a, b, precision=lax.Precision.HIGH, preferred_element_type=jnp.float32)


def on_device(coords, wave, col_factor, counts, blocks, inverse_first, inverse_second):
    row_count = lax.axis_size("row")
    mode_index = lax.axis_index("mode")
    row_index = lax.axis_index("row")
    col_index = lax.axis_index("col")
    block = inverse_first.shape[0]
    width = col_factor.shape[2]
    rows_dev = coords.shape[1] // (lax.axis_size("mode") * row_count)
    assert rows_dev == block and 2 * width == block
    group = mode_index * row_count + row_index

    factor = lax.all_gather(col_factor, "mode", axis=1, tiled=True)

    half = col_index % 2
    col_start = jnp.take(blocks, col_index // 2) * block + half * width
    points = col_start + jnp.arange(width, dtype=jnp.int32)
    xc = lax.dynamic_slice_in_dim(coords[0], col_start, width, 0)
    yc = lax.dynamic_slice_in_dim(coords[1], col_start, width, 0)

    own_start = group * rows_dev
    own_scale = jnp.take(counts, group).astype(jnp.float32) / QMAX
    xr = lax.dynamic_slice_in_dim(coords[0], own_start, rows_dev, 0)
    yr = lax.dynamic_slice_in_dim(coords[1], own_start, rows_dev, 0)
    pivot_block = blocks[0]
    pivot_start = pivot_block * block
    pivot_scale = jnp.take(counts, pivot_block).astype(jnp.float32) / QMAX
    xp = lax.dynamic_slice_in_dim(coords[0], pivot_start, block, 0)
    yp = lax.dynamic_slice_in_dim(coords[1], pivot_start, block, 0)

    own_waves = make_waves(xr, yr, wave)
    pivot_waves = make_waves(xp, yp, wave)

    right = col_index >= 2
    out_cols = half * width
    s_mine = half * width
    s_other = width - s_mine
    inv = lax.dynamic_slice_in_dim(jnp.where(right, inverse_second, inverse_first), out_cols, width, 1)

    def rows_of(mat, start):
        return lax.dynamic_slice_in_dim(mat, start, width, 0)

    pivot_tile, pivot_diag = tile_and_diag(pivot_start, block, pivot_scale, xp, yp, xc, yc, points)
    pivot_mine = lax.cond(
        right,
        lambda: wave_product(pivot_waves, factor) + pivot_tile + pivot_diag,
        lambda: jnp.zeros((block, width), jnp.float32),
    )
    pivot_other = lax.ppermute(pivot_mine, "col", [(2, 3), (3, 2)])
    z = lax.cond(
        right,
        lambda: mm(inverse_first, mm(pivot_mine, rows_of(inv, s_mine)) + mm(pivot_other, rows_of(inv, s_other))),
        lambda: jnp.zeros((block, width), jnp.float32),
    )
    own_waves, _ = lax.optimization_barrier((own_waves, z))

    pieces = 2
    size = rows_dev // pieces
    panel_parts = []
    for p in range(pieces):
        start = p * size
        tile, diag = tile_and_diag(
            own_start + start, size, own_scale, xr[start:start + size], yr[start:start + size], xc, yc, points
        )
        panel_parts.append(wave_product(own_waves, factor, start, size) + tile + diag)
    panel_own = jnp.concatenate(panel_parts, 0)

    swap = [(0, 1), (1, 0), (2, 3), (3, 2)]
    right_swap = [(2, 3), (3, 2)]
    other = lax.ppermute(panel_own, "col", swap)
    first_a = [lax.ppermute(part, "col", [(0, 2), (1, 3)]) for part in panel_parts]
    first_b = [lax.ppermute(part, "col", right_swap) for part in first_a]

    direct = mm(panel_own, rows_of(inv, s_mine)) + mm(other, rows_of(inv, s_other))

    size = rows_dev // len(panel_parts)
    outs = []
    for p in range(len(panel_parts)):
        direct_p = direct[p * size:(p + 1) * size]

        def left_side(direct_p=direct_p):
            return direct_p

        def right_side(direct_p=direct_p, p=p):
            correction = mm_high(first_a[p], rows_of(z, s_mine)) + mm_high(first_b[p], rows_of(z, s_other))
            return direct_p - correction

        outs.append(lax.cond(col_index < 2, left_side, right_side))
    return jnp.concatenate(outs, 0)


def solution(mesh):
    return jax.shard_map(
        on_device,
        mesh=mesh,
        in_specs=(P(), P(), P(None, "mode", "col"), P(), P(), P(), P()),
        out_specs=P(("mode", "row"), "col"),
        check_vma=False,
    )
```

```python
import jax
import jax.numpy as jnp
from jax import lax
from jax.sharding import PartitionSpec as P

QMAX = 8


screen_rate = 6.0
bloch_phase = 0.7
real_amplitude = 0.15
identity_weight = 0.5

HIGHEST = lax.Precision.HIGHEST


def real_part(xr, yr, xc, yc):
    dx = xr[:, None] - xc[None, :]
    dy = yr[:, None] - yc[None, :]
    total = jnp.zeros(dx.shape, jnp.float32)
    for shift in (-1, 0, 1):
        total = total + jnp.cos(jnp.float32(bloch_phase * shift)) * jnp.exp(
            -screen_rate * ((dx - shift) ** 2 + dy * dy)
        )
    return total


HALF_PI_PARTS = (1.5703125, 4.837512969970703125e-4, 7.54978995489188216e-8)
TWO_OVER_PI = 0.6366197723675814
SIN_COEFFS = (-1.9515295891e-4, 8.3321608736e-3, -1.6666654611e-1)
COS_COEFFS = (2.443315711809948e-5, -1.388731625493765e-3, 4.166664568298827e-2)


def cos_and_negsin(theta):
    f32 = jnp.float32
    k = jnp.round(theta * f32(TWO_OVER_PI))
    r = theta
    for part in HALF_PI_PARTS:
        r = r - k * f32(part)
    z = r * r
    s = ((f32(SIN_COEFFS[0]) * z + f32(SIN_COEFFS[1])) * z + f32(SIN_COEFFS[2])) * z * r + r
    c = ((f32(COS_COEFFS[0]) * z + f32(COS_COEFFS[1])) * z + f32(COS_COEFFS[2])) * z * z
    c = c - f32(0.5) * z + f32(1.0)
    quadrant = k - f32(4.0) * jnp.floor(k * f32(0.25))
    odd = (quadrant == 1.0) | (quadrant == 3.0)
    sin_r = jnp.where(odd, c, s)
    cos_r = jnp.where(odd, s, c)
    cos_theta = jnp.where((quadrant == 1.0) | (quadrant == 2.0), -cos_r, cos_r)
    negsin_theta = jnp.where(quadrant >= 2.0, sin_r, -sin_r)
    return cos_theta, negsin_theta


def spectral_rows(xr, yr, wave, factor, pieces=1):
    theta = xr[:, None] * wave[0][None, :] + yr[:, None] * wave[1][None, :]
    cos_theta, negsin_theta = cos_and_negsin(theta)
    cos_part = cos_theta.astype(jnp.bfloat16)
    sin_part = negsin_theta.astype(jnp.bfloat16)
    cos_part, sin_part = lax.optimization_barrier((cos_part, sin_part))
    rows = cos_part.shape[0] // pieces
    out = []
    for p in range(pieces):
        spec = jnp.dot(cos_part[p * rows:(p + 1) * rows], factor[0], preferred_element_type=jnp.float32)
        out.append(spec + jnp.dot(sin_part[p * rows:(p + 1) * rows], factor[1], preferred_element_type=jnp.float32))
    return out if pieces > 1 else out[0]


def panel_rows(start, count, scale, coords, wave, factor, xc, yc, points, pieces=1):
    xr = lax.dynamic_slice_in_dim(coords[0], start, count, 0)
    yr = lax.dynamic_slice_in_dim(coords[1], start, count, 0)
    spectral = spectral_rows(xr, yr, wave, factor, pieces)
    if pieces == 1:
        spectral = [spectral]
    size = count // pieces
    out = []
    for p, spec in enumerate(spectral):
        rows = start + p * size + jnp.arange(size, dtype=jnp.int32)
        xs, ys = xr[p * size:(p + 1) * size], yr[p * size:(p + 1) * size]
        tile = real_amplitude * scale * real_part(xs, ys, xc, yc)
        diag = jnp.where(
            rows[:, None] == points[None, :], jnp.float32(identity_weight), jnp.float32(0.0)
        )
        tile, diag = lax.optimization_barrier((tile, diag))
        out.append(spec + tile + diag)
    return out if pieces > 1 else out[0]


def mm(a, b):
    return jnp.dot(a, b, precision=HIGHEST, preferred_element_type=jnp.float32)


def mm_high(a, b):
    return jnp.dot(a, b, precision=lax.Precision.HIGH, preferred_element_type=jnp.float32)


def on_device(coords, wave, col_factor, counts, blocks, inverse_first, inverse_second):
    row_count = lax.axis_size("row")
    mode_index = lax.axis_index("mode")
    row_index = lax.axis_index("row")
    col_index = lax.axis_index("col")
    block = inverse_first.shape[0]
    width = col_factor.shape[2]
    rows_dev = coords.shape[1] // (lax.axis_size("mode") * row_count)
    assert rows_dev == block and 2 * width == block
    group = mode_index * row_count + row_index

    factor = lax.all_gather(col_factor, "mode", axis=1, tiled=True)

    half = col_index % 2
    col_start = jnp.take(blocks, col_index // 2) * block + half * width
    points = col_start + jnp.arange(width, dtype=jnp.int32)
    xc = lax.dynamic_slice_in_dim(coords[0], col_start, width, 0)
    yc = lax.dynamic_slice_in_dim(coords[1], col_start, width, 0)

    own_start = group * rows_dev
    own_scale = jnp.take(counts, group).astype(jnp.float32) / QMAX
    panel_parts = panel_rows(own_start, rows_dev, own_scale, coords, wave, factor, xc, yc, points, 2)
    panel_own = jnp.concatenate(panel_parts, 0)

    pivot_block = blocks[0]
    pivot_scale = jnp.take(counts, pivot_block).astype(jnp.float32) / QMAX
    pivot_mine = panel_rows(pivot_block * block, block, pivot_scale, coords, wave, factor, xc, yc, points)

    swap = [(0, 1), (1, 0), (2, 3), (3, 2)]
    right_swap = [(2, 3), (3, 2)]
    other = lax.ppermute(panel_own, "col", swap)
    pivot_other = lax.ppermute(pivot_mine, "col", right_swap)
    first_a = [lax.ppermute(part, "col", [(0, 2), (1, 3)]) for part in panel_parts]

    s_mine = half * width
    s_other = width - s_mine
    out_cols = half * width

    def rows_of(mat, start):
        return lax.dynamic_slice_in_dim(mat, start, width, 0)

    inverse = jnp.where(col_index < 2, inverse_first, inverse_second)
    inv = lax.dynamic_slice_in_dim(inverse, out_cols, width, 1)
    direct = mm(panel_own, rows_of(inv, s_mine)) + mm(other, rows_of(inv, s_other))
    q = mm(pivot_mine, rows_of(inv, s_mine)) + mm(pivot_other, rows_of(inv, s_other))
    z = mm(inverse_first, q)
    last = lax.optimization_barrier((first_a[-1], z))[0]
    first_b = [lax.ppermute(part, "col", right_swap) for part in first_a[:-1] + [last]]

    size = rows_dev // len(panel_parts)
    outs = []
    for p in range(len(panel_parts)):
        direct_p = direct[p * size:(p + 1) * size]

        def left_side(direct_p=direct_p):
            return direct_p

        def right_side(direct_p=direct_p, p=p):
            correction = mm_high(first_a[p], rows_of(z, s_mine)) + mm_high(first_b[p], rows_of(z, s_other))
            return direct_p - correction

        outs.append(lax.cond(col_index < 2, left_side, right_side))
    return jnp.concatenate(outs, 0)


def solution(mesh):
    return jax.shard_map(
        on_device,
        mesh=mesh,
        in_specs=(P(), P(), P(None, "mode", "col"), P(), P(), P(), P()),
        out_specs=P(("mode", "row"), "col"),
        check_vma=False,
    )
```

```python
import jax
import jax.numpy as jnp
from jax import lax
from jax.sharding import PartitionSpec as P

QMAX = 8


screen_rate = 6.0
bloch_phase = 0.7
real_amplitude = 0.15
identity_weight = 0.5

HIGHEST = lax.Precision.HIGHEST


def real_part(xr, yr, xc, yc):
    dx = xr[:, None] - xc[None, :]
    dy = yr[:, None] - yc[None, :]
    total = jnp.zeros(dx.shape, jnp.float32)
    for shift in (-1, 0, 1):
        total = total + jnp.cos(jnp.float32(bloch_phase * shift)) * jnp.exp(
            -screen_rate * ((dx - shift) ** 2 + dy * dy)
        )
    return total


HALF_PI_PARTS = (1.5703125, 4.837512969970703125e-4, 7.54978995489188216e-8)
TWO_OVER_PI = 0.6366197723675814
SIN_COEFFS = (-1.9515295891e-4, 8.3321608736e-3, -1.6666654611e-1)
COS_COEFFS = (2.443315711809948e-5, -1.388731625493765e-3, 4.166664568298827e-2)


def cos_and_negsin(theta):
    f32 = jnp.float32
    k = jnp.round(theta * f32(TWO_OVER_PI))
    r = theta
    for part in HALF_PI_PARTS:
        r = r - k * f32(part)
    z = r * r
    s = ((f32(SIN_COEFFS[0]) * z + f32(SIN_COEFFS[1])) * z + f32(SIN_COEFFS[2])) * z * r + r
    c = ((f32(COS_COEFFS[0]) * z + f32(COS_COEFFS[1])) * z + f32(COS_COEFFS[2])) * z * z
    c = c - f32(0.5) * z + f32(1.0)
    quadrant = k - f32(4.0) * jnp.floor(k * f32(0.25))
    odd = (quadrant == 1.0) | (quadrant == 3.0)
    sin_r = jnp.where(odd, c, s)
    cos_r = jnp.where(odd, s, c)
    cos_theta = jnp.where((quadrant == 1.0) | (quadrant == 2.0), -cos_r, cos_r)
    negsin_theta = jnp.where(quadrant >= 2.0, sin_r, -sin_r)
    return cos_theta, negsin_theta


def spectral_rows(xr, yr, wave, factor, pieces=1):
    theta = xr[:, None] * wave[0][None, :] + yr[:, None] * wave[1][None, :]
    cos_theta, negsin_theta = cos_and_negsin(theta)
    cos_part = cos_theta.astype(jnp.bfloat16)
    sin_part = negsin_theta.astype(jnp.bfloat16)
    cos_part, sin_part = lax.optimization_barrier((cos_part, sin_part))
    rows = cos_part.shape[0] // pieces
    out = []
    for p in range(pieces):
        spec = jnp.dot(cos_part[p * rows:(p + 1) * rows], factor[0], preferred_element_type=jnp.float32)
        out.append(spec + jnp.dot(sin_part[p * rows:(p + 1) * rows], factor[1], preferred_element_type=jnp.float32))
    return out if pieces > 1 else out[0]


def panel_rows(start, count, scale, coords, wave, factor, xc, yc, points, pieces=1):
    xr = lax.dynamic_slice_in_dim(coords[0], start, count, 0)
    yr = lax.dynamic_slice_in_dim(coords[1], start, count, 0)
    spectral = spectral_rows(xr, yr, wave, factor, pieces)
    if pieces == 1:
        spectral = [spectral]
    size = count // pieces
    out = []
    for p, spec in enumerate(spectral):
        rows = start + p * size + jnp.arange(size, dtype=jnp.int32)
        xs, ys = xr[p * size:(p + 1) * size], yr[p * size:(p + 1) * size]
        tile = real_amplitude * scale * real_part(xs, ys, xc, yc)
        diag = jnp.where(
            rows[:, None] == points[None, :], jnp.float32(identity_weight), jnp.float32(0.0)
        )
        tile, diag = lax.optimization_barrier((tile, diag))
        out.append(spec + tile + diag)
    return out if pieces > 1 else out[0]


def mm(a, b):
    return jnp.dot(a, b, precision=HIGHEST, preferred_element_type=jnp.float32)


def mm_high(a, b):
    return jnp.dot(a, b, precision=lax.Precision.HIGH, preferred_element_type=jnp.float32)


def on_device(coords, wave, col_factor, counts, blocks, inverse_first, inverse_second):
    row_count = lax.axis_size("row")
    mode_index = lax.axis_index("mode")
    row_index = lax.axis_index("row")
    col_index = lax.axis_index("col")
    block = inverse_first.shape[0]
    width = col_factor.shape[2]
    rows_dev = coords.shape[1] // (lax.axis_size("mode") * row_count)
    assert rows_dev == block and 2 * width == block
    group = mode_index * row_count + row_index

    factor = lax.all_gather(col_factor, "mode", axis=1, tiled=True)

    half = col_index % 2
    col_start = jnp.take(blocks, col_index // 2) * block + half * width
    points = col_start + jnp.arange(width, dtype=jnp.int32)
    xc = lax.dynamic_slice_in_dim(coords[0], col_start, width, 0)
    yc = lax.dynamic_slice_in_dim(coords[1], col_start, width, 0)

    own_start = group * rows_dev
    own_scale = jnp.take(counts, group).astype(jnp.float32) / QMAX
    panel_parts = panel_rows(own_start, rows_dev, own_scale, coords, wave, factor, xc, yc, points, 4)
    panel_own = jnp.concatenate(panel_parts, 0)

    pivot_block = blocks[0]
    pivot_scale = jnp.take(counts, pivot_block).astype(jnp.float32) / QMAX
    pivot_mine = panel_rows(pivot_block * block, block, pivot_scale, coords, wave, factor, xc, yc, points)

    swap = [(0, 1), (1, 0), (2, 3), (3, 2)]
    right_swap = [(2, 3), (3, 2)]
    other = lax.ppermute(panel_own, "col", swap)
    pivot_other = lax.ppermute(pivot_mine, "col", right_swap)
    first_a = [lax.ppermute(part, "col", [(0, 2), (1, 3)]) for part in panel_parts]

    s_mine = half * width
    s_other = width - s_mine
    out_cols = half * width

    def rows_of(mat, start):
        return lax.dynamic_slice_in_dim(mat, start, width, 0)

    inverse = jnp.where(col_index < 2, inverse_first, inverse_second)
    inv = lax.dynamic_slice_in_dim(inverse, out_cols, width, 1)
    direct = mm(panel_own, rows_of(inv, s_mine)) + mm(other, rows_of(inv, s_other))
    q = mm(pivot_mine, rows_of(inv, s_mine)) + mm(pivot_other, rows_of(inv, s_other))
    z = mm(inverse_first, q)
    last = lax.optimization_barrier((first_a[-1], z))[0]
    first_b = [lax.ppermute(part, "col", right_swap) for part in first_a[:-1] + [last]]

    size = rows_dev // len(panel_parts)
    outs = []
    for p in range(len(panel_parts)):
        direct_p = direct[p * size:(p + 1) * size]

        def left_side(direct_p=direct_p):
            return direct_p

        def right_side(direct_p=direct_p, p=p):
            correction = mm_high(first_a[p], rows_of(z, s_mine)) + mm_high(first_b[p], rows_of(z, s_other))
            return direct_p - correction

        outs.append(lax.cond(col_index < 2, left_side, right_side))
    return jnp.concatenate(outs, 0)


def solution(mesh):
    return jax.shard_map(
        on_device,
        mesh=mesh,
        in_specs=(P(), P(), P(None, "mode", "col"), P(), P(), P(), P()),
        out_specs=P(("mode", "row"), "col"),
        check_vma=False,
    )
```

```python
import jax
import jax.numpy as jnp
from jax import lax
from jax.sharding import PartitionSpec as P

QMAX = 8


screen_rate = 6.0
bloch_phase = 0.7
real_amplitude = 0.15
identity_weight = 0.5

HIGHEST = lax.Precision.HIGHEST


def real_part(xr, yr, xc, yc):
    dx = xr[:, None] - xc[None, :]
    dy = yr[:, None] - yc[None, :]
    total = jnp.zeros(dx.shape, jnp.float32)
    for shift in (-1, 0, 1):
        total = total + jnp.cos(jnp.float32(bloch_phase * shift)) * jnp.exp(
            -screen_rate * ((dx - shift) ** 2 + dy * dy)
        )
    return total


HALF_PI_PARTS = (1.5703125, 4.837512969970703125e-4, 7.54978995489188216e-8)
TWO_OVER_PI = 0.6366197723675814
SIN_COEFFS = (-1.9515295891e-4, 8.3321608736e-3, -1.6666654611e-1)
COS_COEFFS = (2.443315711809948e-5, -1.388731625493765e-3, 4.166664568298827e-2)


def cos_and_negsin(theta):
    f32 = jnp.float32
    k = jnp.round(theta * f32(TWO_OVER_PI))
    r = theta
    for part in HALF_PI_PARTS:
        r = r - k * f32(part)
    z = r * r
    s = ((f32(SIN_COEFFS[0]) * z + f32(SIN_COEFFS[1])) * z + f32(SIN_COEFFS[2])) * z * r + r
    c = ((f32(COS_COEFFS[0]) * z + f32(COS_COEFFS[1])) * z + f32(COS_COEFFS[2])) * z * z
    c = c - f32(0.5) * z + f32(1.0)
    quadrant = k - f32(4.0) * jnp.floor(k * f32(0.25))
    odd = (quadrant == 1.0) | (quadrant == 3.0)
    sin_r = jnp.where(odd, c, s)
    cos_r = jnp.where(odd, s, c)
    cos_theta = jnp.where((quadrant == 1.0) | (quadrant == 2.0), -cos_r, cos_r)
    negsin_theta = jnp.where(quadrant >= 2.0, sin_r, -sin_r)
    return cos_theta, negsin_theta


def make_waves(xr, yr, wave):
    theta = xr[:, None] * wave[0][None, :] + yr[:, None] * wave[1][None, :]
    cos_theta, negsin_theta = cos_and_negsin(theta)
    cos_part = cos_theta.astype(jnp.bfloat16)
    sin_part = negsin_theta.astype(jnp.bfloat16)
    return lax.optimization_barrier((cos_part, sin_part))


def spectral_rows(xr, yr, wave, factor, pieces=1, waves=None):
    cos_part, sin_part = make_waves(xr, yr, wave) if waves is None else waves
    rows = cos_part.shape[0] // pieces
    out = []
    for p in range(pieces):
        spec = jnp.dot(cos_part[p * rows:(p + 1) * rows], factor[0], preferred_element_type=jnp.float32)
        out.append(spec + jnp.dot(sin_part[p * rows:(p + 1) * rows], factor[1], preferred_element_type=jnp.float32))
    return out if pieces > 1 else out[0]


def panel_rows(start, count, scale, coords, wave, factor, xc, yc, points, pieces=1):
    xr = lax.dynamic_slice_in_dim(coords[0], start, count, 0)
    yr = lax.dynamic_slice_in_dim(coords[1], start, count, 0)
    spectral = spectral_rows(xr, yr, wave, factor, pieces)
    if pieces == 1:
        spectral = [spectral]
    size = count // pieces
    out = []
    for p, spec in enumerate(spectral):
        rows = start + p * size + jnp.arange(size, dtype=jnp.int32)
        xs, ys = xr[p * size:(p + 1) * size], yr[p * size:(p + 1) * size]
        tile = real_amplitude * scale * real_part(xs, ys, xc, yc)
        diag = jnp.where(
            rows[:, None] == points[None, :], jnp.float32(identity_weight), jnp.float32(0.0)
        )
        tile, diag = lax.optimization_barrier((tile, diag))
        out.append(spec + tile + diag)
    return out if pieces > 1 else out[0]


def mm(a, b):
    return jnp.dot(a, b, precision=HIGHEST, preferred_element_type=jnp.float32)


def mm_high(a, b):
    return jnp.dot(a, b, precision=lax.Precision.HIGH, preferred_element_type=jnp.float32)


def on_device(coords, wave, col_factor, counts, blocks, inverse_first, inverse_second):
    row_count = lax.axis_size("row")
    mode_index = lax.axis_index("mode")
    row_index = lax.axis_index("row")
    col_index = lax.axis_index("col")
    block = inverse_first.shape[0]
    width = col_factor.shape[2]
    rows_dev = coords.shape[1] // (lax.axis_size("mode") * row_count)
    assert rows_dev == block and 2 * width == block
    group = mode_index * row_count + row_index

    factor = lax.all_gather(col_factor, "mode", axis=1, tiled=True)

    half = col_index % 2
    col_start = jnp.take(blocks, col_index // 2) * block + half * width
    points = col_start + jnp.arange(width, dtype=jnp.int32)
    xc = lax.dynamic_slice_in_dim(coords[0], col_start, width, 0)
    yc = lax.dynamic_slice_in_dim(coords[1], col_start, width, 0)

    own_start = group * rows_dev
    own_scale = jnp.take(counts, group).astype(jnp.float32) / QMAX
    panel_parts = panel_rows(own_start, rows_dev, own_scale, coords, wave, factor, xc, yc, points, 2)
    panel_own = jnp.concatenate(panel_parts, 0)

    pivot_block = blocks[0]
    pivot_scale = jnp.take(counts, pivot_block).astype(jnp.float32) / QMAX
    pivot_start = pivot_block * block
    xp = lax.dynamic_slice_in_dim(coords[0], pivot_start, block, 0)
    yp = lax.dynamic_slice_in_dim(coords[1], pivot_start, block, 0)
    pivot_waves = make_waves(xp, yp, wave)
    pivot_rows = pivot_start + jnp.arange(block, dtype=jnp.int32)
    pivot_tile = real_amplitude * pivot_scale * real_part(xp, yp, xc, yc)
    pivot_diag = jnp.where(
        pivot_rows[:, None] == points[None, :], jnp.float32(identity_weight), jnp.float32(0.0)
    )
    pivot_tile, pivot_diag = lax.optimization_barrier((pivot_tile, pivot_diag))
    pivot_mine = lax.cond(
        col_index >= 2,
        lambda: spectral_rows(xp, yp, wave, factor, waves=pivot_waves) + pivot_tile + pivot_diag,
        lambda: jnp.zeros((block, width), jnp.float32),
    )

    swap = [(0, 1), (1, 0), (2, 3), (3, 2)]
    right_swap = [(2, 3), (3, 2)]
    other = lax.ppermute(panel_own, "col", swap)
    pivot_other = lax.ppermute(pivot_mine, "col", right_swap)
    first_a = [lax.ppermute(part, "col", [(0, 2), (1, 3)]) for part in panel_parts]

    s_mine = half * width
    s_other = width - s_mine
    out_cols = half * width

    def rows_of(mat, start):
        return lax.dynamic_slice_in_dim(mat, start, width, 0)

    inverse = jnp.where(col_index < 2, inverse_first, inverse_second)
    inv = lax.dynamic_slice_in_dim(inverse, out_cols, width, 1)
    direct = mm(panel_own, rows_of(inv, s_mine)) + mm(other, rows_of(inv, s_other))
    q = mm(pivot_mine, rows_of(inv, s_mine)) + mm(pivot_other, rows_of(inv, s_other))
    z = mm(inverse_first, q)
    last = lax.optimization_barrier((first_a[-1], z))[0]
    first_b = [lax.ppermute(part, "col", right_swap) for part in first_a[:-1] + [last]]

    size = rows_dev // len(panel_parts)
    outs = []
    for p in range(len(panel_parts)):
        direct_p = direct[p * size:(p + 1) * size]

        def left_side(direct_p=direct_p):
            return direct_p

        def right_side(direct_p=direct_p, p=p):
            correction = mm_high(first_a[p], rows_of(z, s_mine)) + mm_high(first_b[p], rows_of(z, s_other))
            return direct_p - correction

        outs.append(lax.cond(col_index < 2, left_side, right_side))
    return jnp.concatenate(outs, 0)


def solution(mesh):
    return jax.shard_map(
        on_device,
        mesh=mesh,
        in_specs=(P(), P(), P(None, "mode", "col"), P(), P(), P(), P()),
        out_specs=P(("mode", "row"), "col"),
        check_vma=False,
    )
```

```python
import jax
import jax.numpy as jnp
from jax import lax
from jax.sharding import PartitionSpec as P

QMAX = 8


screen_rate = 6.0
bloch_phase = 0.7
real_amplitude = 0.15
identity_weight = 0.5

HIGHEST = lax.Precision.HIGHEST


def real_part(xr, yr, xc, yc):
    dx = xr[:, None] - xc[None, :]
    dy = yr[:, None] - yc[None, :]
    total = jnp.zeros(dx.shape, jnp.float32)
    for shift in (-1, 0, 1):
        total = total + jnp.cos(jnp.float32(bloch_phase * shift)) * jnp.exp(
            -screen_rate * ((dx - shift) ** 2 + dy * dy)
        )
    return total


HALF_PI_PARTS = (1.5703125, 4.837512969970703125e-4, 7.54978995489188216e-8)
TWO_OVER_PI = 0.6366197723675814
SIN_COEFFS = (-1.9515295891e-4, 8.3321608736e-3, -1.6666654611e-1)
COS_COEFFS = (2.443315711809948e-5, -1.388731625493765e-3, 4.166664568298827e-2)


def cos_and_negsin(theta):
    f32 = jnp.float32
    k = jnp.round(theta * f32(TWO_OVER_PI))
    r = theta
    for part in HALF_PI_PARTS:
        r = r - k * f32(part)
    z = r * r
    s = ((f32(SIN_COEFFS[0]) * z + f32(SIN_COEFFS[1])) * z + f32(SIN_COEFFS[2])) * z * r + r
    c = ((f32(COS_COEFFS[0]) * z + f32(COS_COEFFS[1])) * z + f32(COS_COEFFS[2])) * z * z
    c = c - f32(0.5) * z + f32(1.0)
    quadrant = k - f32(4.0) * jnp.floor(k * f32(0.25))
    odd = (quadrant == 1.0) | (quadrant == 3.0)
    sin_r = jnp.where(odd, c, s)
    cos_r = jnp.where(odd, s, c)
    cos_theta = jnp.where((quadrant == 1.0) | (quadrant == 2.0), -cos_r, cos_r)
    negsin_theta = jnp.where(quadrant >= 2.0, sin_r, -sin_r)
    return cos_theta, negsin_theta


def spectral_rows(xr, yr, wave, factor, pieces=1):
    theta = xr[:, None] * wave[0][None, :] + yr[:, None] * wave[1][None, :]
    cos_theta, negsin_theta = cos_and_negsin(theta)
    cos_part = cos_theta.astype(jnp.bfloat16)
    sin_part = negsin_theta.astype(jnp.bfloat16)
    cos_part, sin_part = lax.optimization_barrier((cos_part, sin_part))
    rows = cos_part.shape[0] // pieces
    out = []
    for p in range(pieces):
        spec = jnp.dot(cos_part[p * rows:(p + 1) * rows], factor[0], preferred_element_type=jnp.float32)
        out.append(spec + jnp.dot(sin_part[p * rows:(p + 1) * rows], factor[1], preferred_element_type=jnp.float32))
    return out if pieces > 1 else out[0]


def panel_rows(start, count, scale, coords, wave, factor, xc, yc, points, pieces=1):
    xr = lax.dynamic_slice_in_dim(coords[0], start, count, 0)
    yr = lax.dynamic_slice_in_dim(coords[1], start, count, 0)
    spectral = spectral_rows(xr, yr, wave, factor, pieces)
    if pieces == 1:
        spectral = [spectral]
    size = count // pieces
    out = []
    for p, spec in enumerate(spectral):
        rows = start + p * size + jnp.arange(size, dtype=jnp.int32)
        xs, ys = xr[p * size:(p + 1) * size], yr[p * size:(p + 1) * size]
        tile = real_amplitude * scale * real_part(xs, ys, xc, yc)
        diag = jnp.where(
            rows[:, None] == points[None, :], jnp.float32(identity_weight), jnp.float32(0.0)
        )
        tile, diag = lax.optimization_barrier((tile, diag))
        out.append(spec + tile + diag)
    return out if pieces > 1 else out[0]


def mm(a, b):
    return jnp.dot(a, b, precision=HIGHEST, preferred_element_type=jnp.float32)


def mm_high(a, b):
    return jnp.dot(a, b, precision=lax.Precision.HIGH, preferred_element_type=jnp.float32)


def on_device(coords, wave, col_factor, counts, blocks, inverse_first, inverse_second):
    row_count = lax.axis_size("row")
    mode_index = lax.axis_index("mode")
    row_index = lax.axis_index("row")
    col_index = lax.axis_index("col")
    block = inverse_first.shape[0]
    width = col_factor.shape[2]
    rows_dev = coords.shape[1] // (lax.axis_size("mode") * row_count)
    assert rows_dev == block and 2 * width == block
    group = mode_index * row_count + row_index

    factor = lax.all_gather(col_factor, "mode", axis=1, tiled=True)

    half = col_index % 2
    col_start = jnp.take(blocks, col_index // 2) * block + half * width
    points = col_start + jnp.arange(width, dtype=jnp.int32)
    xc = lax.dynamic_slice_in_dim(coords[0], col_start, width, 0)
    yc = lax.dynamic_slice_in_dim(coords[1], col_start, width, 0)

    own_start = group * rows_dev
    own_scale = jnp.take(counts, group).astype(jnp.float32) / QMAX
    panel_parts = panel_rows(own_start, rows_dev, own_scale, coords, wave, factor, xc, yc, points, 2)
    panel_own = jnp.concatenate(panel_parts, 0)

    pivot_block = blocks[0]
    pivot_scale = jnp.take(counts, pivot_block).astype(jnp.float32) / QMAX
    pivot_mine = panel_rows(pivot_block * block, block, pivot_scale, coords, wave, factor, xc, yc, points)

    swap = [(0, 1), (1, 0), (2, 3), (3, 2)]
    right_swap = [(2, 3), (3, 2)]
    other = lax.ppermute(panel_own, "col", swap)
    pivot_other = lax.ppermute(pivot_mine, "col", right_swap)
    first_a = [lax.ppermute(part, "col", [(0, 2), (1, 3)]) for part in panel_parts]

    s_mine = half * width
    s_other = width - s_mine
    out_cols = half * width

    def rows_of(mat, start):
        return lax.dynamic_slice_in_dim(mat, start, width, 0)

    inverse = jnp.where(col_index < 2, inverse_first, inverse_second)
    inv = lax.dynamic_slice_in_dim(inverse, out_cols, width, 1)
    direct = mm(panel_own, rows_of(inv, s_mine)) + mm(other, rows_of(inv, s_other))
    q = mm(pivot_mine, rows_of(inv, s_mine)) + mm(pivot_other, rows_of(inv, s_other))
    z = mm(inverse_first, q)
    size = rows_dev // len(panel_parts)

    def corrected(p, a_part, b_part):
        direct_p = direct[p * size:(p + 1) * size]

        def left_side():
            return direct_p

        def right_side():
            correction = mm_high(a_part, rows_of(z, s_mine)) + mm_high(b_part, rows_of(z, s_other))
            return direct_p - correction

        return lax.cond(col_index < 2, left_side, right_side)

    outs = []
    for p, a_part in enumerate(first_a):
        if p > 0:
            a_part = lax.optimization_barrier((a_part, z, outs[-1]))[0]
        b_part = lax.ppermute(a_part, "col", right_swap)
        outs.append(corrected(p, first_a[p], b_part))
    return jnp.concatenate(outs, 0)


def solution(mesh):
    return jax.shard_map(
        on_device,
        mesh=mesh,
        in_specs=(P(), P(), P(None, "mode", "col"), P(), P(), P(), P()),
        out_specs=P(("mode", "row"), "col"),
        check_vma=False,
    )
```

```python
import jax
import jax.numpy as jnp
from jax import lax
from jax.sharding import PartitionSpec as P

QMAX = 8


screen_rate = 6.0
bloch_phase = 0.7
real_amplitude = 0.15
identity_weight = 0.5

HIGHEST = lax.Precision.HIGHEST


def real_part(xr, yr, xc, yc):
    dx = xr[:, None] - xc[None, :]
    dy = yr[:, None] - yc[None, :]
    total = jnp.zeros(dx.shape, jnp.float32)
    for shift in (-1, 0, 1):
        total = total + jnp.cos(jnp.float32(bloch_phase * shift)) * jnp.exp(
            -screen_rate * ((dx - shift) ** 2 + dy * dy)
        )
    return total


HALF_PI_PARTS = (1.5703125, 4.837512969970703125e-4, 7.54978995489188216e-8)
TWO_OVER_PI = 0.6366197723675814
SIN_COEFFS = (-1.9515295891e-4, 8.3321608736e-3, -1.6666654611e-1)
COS_COEFFS = (2.443315711809948e-5, -1.388731625493765e-3, 4.166664568298827e-2)


def cos_and_negsin(theta):
    f32 = jnp.float32
    k = jnp.round(theta * f32(TWO_OVER_PI))
    r = theta
    for part in HALF_PI_PARTS:
        r = r - k * f32(part)
    z = r * r
    s = ((f32(SIN_COEFFS[0]) * z + f32(SIN_COEFFS[1])) * z + f32(SIN_COEFFS[2])) * z * r + r
    c = ((f32(COS_COEFFS[0]) * z + f32(COS_COEFFS[1])) * z + f32(COS_COEFFS[2])) * z * z
    c = c - f32(0.5) * z + f32(1.0)
    quadrant = k - f32(4.0) * jnp.floor(k * f32(0.25))
    odd = (quadrant == 1.0) | (quadrant == 3.0)
    sin_r = jnp.where(odd, c, s)
    cos_r = jnp.where(odd, s, c)
    cos_theta = jnp.where((quadrant == 1.0) | (quadrant == 2.0), -cos_r, cos_r)
    negsin_theta = jnp.where(quadrant >= 2.0, sin_r, -sin_r)
    return cos_theta, negsin_theta


def spectral_rows(xr, yr, wave, factor, splits=None):
    theta = xr[:, None] * wave[0][None, :] + yr[:, None] * wave[1][None, :]
    cos_theta, negsin_theta = cos_and_negsin(theta)
    cos_part = cos_theta.astype(jnp.bfloat16)
    sin_part = negsin_theta.astype(jnp.bfloat16)
    cos_part, sin_part = lax.optimization_barrier((cos_part, sin_part))
    bounds = row_bounds(cos_part.shape[0], splits)
    out = []
    for lo, hi in bounds:
        spec = jnp.dot(cos_part[lo:hi], factor[0], preferred_element_type=jnp.float32)
        out.append(spec + jnp.dot(sin_part[lo:hi], factor[1], preferred_element_type=jnp.float32))
    return out


def row_bounds(count, splits):
    splits = [count] if splits is None else splits
    assert sum(splits) == count
    starts = [sum(splits[:i]) for i in range(len(splits))]
    return [(a, a + n) for a, n in zip(starts, splits)]


def panel_rows(start, count, scale, coords, wave, factor, xc, yc, points, splits=None):
    xr = lax.dynamic_slice_in_dim(coords[0], start, count, 0)
    yr = lax.dynamic_slice_in_dim(coords[1], start, count, 0)
    spectral = spectral_rows(xr, yr, wave, factor, splits)
    out = []
    for (lo, hi), spec in zip(row_bounds(count, splits), spectral):
        rows = start + lo + jnp.arange(hi - lo, dtype=jnp.int32)
        xs, ys = xr[lo:hi], yr[lo:hi]
        tile = real_amplitude * scale * real_part(xs, ys, xc, yc)
        diag = jnp.where(
            rows[:, None] == points[None, :], jnp.float32(identity_weight), jnp.float32(0.0)
        )
        tile, diag = lax.optimization_barrier((tile, diag))
        out.append(spec + tile + diag)
    return out if splits is not None else out[0]


def mm(a, b):
    return jnp.dot(a, b, precision=HIGHEST, preferred_element_type=jnp.float32)


def mm_high(a, b):
    return jnp.dot(a, b, precision=lax.Precision.HIGH, preferred_element_type=jnp.float32)


def on_device(coords, wave, col_factor, counts, blocks, inverse_first, inverse_second):
    row_count = lax.axis_size("row")
    mode_index = lax.axis_index("mode")
    row_index = lax.axis_index("row")
    col_index = lax.axis_index("col")
    block = inverse_first.shape[0]
    width = col_factor.shape[2]
    rows_dev = coords.shape[1] // (lax.axis_size("mode") * row_count)
    assert rows_dev == block and 2 * width == block
    group = mode_index * row_count + row_index

    factor = lax.all_gather(col_factor, "mode", axis=1, tiled=True)

    half = col_index % 2
    col_start = jnp.take(blocks, col_index // 2) * block + half * width
    points = col_start + jnp.arange(width, dtype=jnp.int32)
    xc = lax.dynamic_slice_in_dim(coords[0], col_start, width, 0)
    yc = lax.dynamic_slice_in_dim(coords[1], col_start, width, 0)

    own_start = group * rows_dev
    own_scale = jnp.take(counts, group).astype(jnp.float32) / QMAX
    splits = [rows_dev * 3 // 4, rows_dev // 4]
    panel_parts = panel_rows(own_start, rows_dev, own_scale, coords, wave, factor, xc, yc, points, splits)
    panel_own = jnp.concatenate(panel_parts, 0)

    pivot_block = blocks[0]
    pivot_scale = jnp.take(counts, pivot_block).astype(jnp.float32) / QMAX
    pivot_mine = panel_rows(pivot_block * block, block, pivot_scale, coords, wave, factor, xc, yc, points)

    swap = [(0, 1), (1, 0), (2, 3), (3, 2)]
    right_swap = [(2, 3), (3, 2)]
    other = lax.ppermute(panel_own, "col", swap)
    pivot_other = lax.ppermute(pivot_mine, "col", right_swap)
    first_a = [lax.ppermute(part, "col", [(0, 2), (1, 3)]) for part in panel_parts]

    s_mine = half * width
    s_other = width - s_mine
    out_cols = half * width

    def rows_of(mat, start):
        return lax.dynamic_slice_in_dim(mat, start, width, 0)

    inverse = jnp.where(col_index < 2, inverse_first, inverse_second)
    inv = lax.dynamic_slice_in_dim(inverse, out_cols, width, 1)
    direct = mm(panel_own, rows_of(inv, s_mine)) + mm(other, rows_of(inv, s_other))
    q = mm(pivot_mine, rows_of(inv, s_mine)) + mm(pivot_other, rows_of(inv, s_other))
    z = mm(inverse_first, q)
    last = lax.optimization_barrier((first_a[-1], z))[0]
    first_b = [lax.ppermute(part, "col", right_swap) for part in first_a[:-1] + [last]]

    outs = []
    for p, (lo, hi) in enumerate(row_bounds(rows_dev, splits)):
        direct_p = direct[lo:hi]

        def left_side(direct_p=direct_p):
            return direct_p

        def right_side(direct_p=direct_p, p=p):
            correction = mm_high(first_a[p], rows_of(z, s_mine)) + mm_high(first_b[p], rows_of(z, s_other))
            return direct_p - correction

        outs.append(lax.cond(col_index < 2, left_side, right_side))
    return jnp.concatenate(outs, 0)


def solution(mesh):
    return jax.shard_map(
        on_device,
        mesh=mesh,
        in_specs=(P(), P(), P(None, "mode", "col"), P(), P(), P(), P()),
        out_specs=P(("mode", "row"), "col"),
        check_vma=False,
    )
```

```python
import jax
import jax.numpy as jnp
from jax import lax
from jax.sharding import PartitionSpec as P

QMAX = 8


screen_rate = 6.0
bloch_phase = 0.7
real_amplitude = 0.15
identity_weight = 0.5

HIGHEST = lax.Precision.HIGHEST


def real_part(xr, yr, xc, yc):
    dx = xr[:, None] - xc[None, :]
    dy = yr[:, None] - yc[None, :]
    total = jnp.zeros(dx.shape, jnp.float32)
    for shift in (-1, 0, 1):
        total = total + jnp.cos(jnp.float32(bloch_phase * shift)) * jnp.exp(
            -screen_rate * ((dx - shift) ** 2 + dy * dy)
        )
    return total


HALF_PI_PARTS = (1.5703125, 4.837512969970703125e-4, 7.54978995489188216e-8)
TWO_OVER_PI = 0.6366197723675814
SIN_COEFFS = (-1.9515295891e-4, 8.3321608736e-3, -1.6666654611e-1)
COS_COEFFS = (2.443315711809948e-5, -1.388731625493765e-3, 4.166664568298827e-2)


def cos_and_negsin(theta):
    f32 = jnp.float32
    k = jnp.round(theta * f32(TWO_OVER_PI))
    r = theta
    for part in HALF_PI_PARTS:
        r = r - k * f32(part)
    z = r * r
    s = ((f32(SIN_COEFFS[0]) * z + f32(SIN_COEFFS[1])) * z + f32(SIN_COEFFS[2])) * z * r + r
    c = ((f32(COS_COEFFS[0]) * z + f32(COS_COEFFS[1])) * z + f32(COS_COEFFS[2])) * z * z
    c = c - f32(0.5) * z + f32(1.0)
    quadrant = k - f32(4.0) * jnp.floor(k * f32(0.25))
    odd = (quadrant == 1.0) | (quadrant == 3.0)
    sin_r = jnp.where(odd, c, s)
    cos_r = jnp.where(odd, s, c)
    cos_theta = jnp.where((quadrant == 1.0) | (quadrant == 2.0), -cos_r, cos_r)
    negsin_theta = jnp.where(quadrant >= 2.0, sin_r, -sin_r)
    return cos_theta, negsin_theta


def spectral_rows(xr, yr, wave, factor, pieces=1):
    theta = xr[:, None] * wave[0][None, :] + yr[:, None] * wave[1][None, :]
    cos_theta, negsin_theta = cos_and_negsin(theta)
    cos_part = cos_theta.astype(jnp.bfloat16)
    sin_part = negsin_theta.astype(jnp.bfloat16)
    cos_part, sin_part = lax.optimization_barrier((cos_part, sin_part))
    rows = cos_part.shape[0] // pieces
    out = []
    for p in range(pieces):
        spec = jnp.dot(cos_part[p * rows:(p + 1) * rows], factor[0], preferred_element_type=jnp.float32)
        out.append(spec + jnp.dot(sin_part[p * rows:(p + 1) * rows], factor[1], preferred_element_type=jnp.float32))
    return out if pieces > 1 else out[0]


def panel_rows(start, count, scale, coords, wave, factor, xc, yc, points, pieces=1):
    xr = lax.dynamic_slice_in_dim(coords[0], start, count, 0)
    yr = lax.dynamic_slice_in_dim(coords[1], start, count, 0)
    spectral = spectral_rows(xr, yr, wave, factor, pieces)
    if pieces == 1:
        spectral = [spectral]
    size = count // pieces
    out = []
    for p, spec in enumerate(spectral):
        rows = start + p * size + jnp.arange(size, dtype=jnp.int32)
        xs, ys = xr[p * size:(p + 1) * size], yr[p * size:(p + 1) * size]
        tile = real_amplitude * scale * real_part(xs, ys, xc, yc)
        diag = jnp.where(
            rows[:, None] == points[None, :], jnp.float32(identity_weight), jnp.float32(0.0)
        )
        tile, diag = lax.optimization_barrier((tile, diag))
        out.append(spec + tile + diag)
    return out if pieces > 1 else out[0]


def mm(a, b):
    return jnp.dot(a, b, precision=HIGHEST, preferred_element_type=jnp.float32)


def mm_high(a, b):
    return jnp.dot(a, b, precision=lax.Precision.HIGH, preferred_element_type=jnp.float32)


def on_device(coords, wave, col_factor, counts, blocks, inverse_first, inverse_second):
    row_count = lax.axis_size("row")
    mode_index = lax.axis_index("mode")
    row_index = lax.axis_index("row")
    col_index = lax.axis_index("col")
    block = inverse_first.shape[0]
    width = col_factor.shape[2]
    rows_dev = coords.shape[1] // (lax.axis_size("mode") * row_count)
    assert rows_dev == block and 2 * width == block
    group = mode_index * row_count + row_index

    factor = lax.all_gather(col_factor, "mode", axis=1, tiled=True)

    half = col_index % 2
    col_start = jnp.take(blocks, col_index // 2) * block + half * width
    points = col_start + jnp.arange(width, dtype=jnp.int32)
    xc = lax.dynamic_slice_in_dim(coords[0], col_start, width, 0)
    yc = lax.dynamic_slice_in_dim(coords[1], col_start, width, 0)

    own_start = group * rows_dev
    own_scale = jnp.take(counts, group).astype(jnp.float32) / QMAX
    panel_parts = panel_rows(own_start, rows_dev, own_scale, coords, wave, factor, xc, yc, points, 2)
    panel_own = jnp.concatenate(panel_parts, 0)

    pivot_block = blocks[0]
    pivot_scale = jnp.take(counts, pivot_block).astype(jnp.float32) / QMAX
    pivot_mine = panel_rows(pivot_block * block, block, pivot_scale, coords, wave, factor, xc, yc, points)

    swap = [(0, 1), (1, 0), (2, 3), (3, 2)]
    right_swap = [(2, 3), (3, 2)]
    other = lax.ppermute(panel_own, "col", swap)
    pivot_other = lax.ppermute(pivot_mine, "col", right_swap)
    first_a = [lax.ppermute(part, "col", [(0, 2), (1, 3)]) for part in panel_parts]

    s_mine = half * width
    s_other = width - s_mine
    out_cols = half * width

    def rows_of(mat, start):
        return lax.dynamic_slice_in_dim(mat, start, width, 0)

    inverse = jnp.where(col_index < 2, inverse_first, inverse_second)
    inv = lax.dynamic_slice_in_dim(inverse, out_cols, width, 1)
    direct = mm_high(panel_own, rows_of(inv, s_mine)) + mm_high(other, rows_of(inv, s_other))
    q = mm_high(pivot_mine, rows_of(inv, s_mine)) + mm_high(pivot_other, rows_of(inv, s_other))
    z = mm_high(inverse_first, q)
    last = lax.optimization_barrier((first_a[-1], z))[0]
    first_b = [lax.ppermute(part, "col", right_swap) for part in first_a[:-1] + [last]]

    size = rows_dev // len(panel_parts)
    outs = []
    for p in range(len(panel_parts)):
        direct_p = direct[p * size:(p + 1) * size]

        def left_side(direct_p=direct_p):
            return direct_p

        def right_side(direct_p=direct_p, p=p):
            correction = mm_high(first_a[p], rows_of(z, s_mine)) + mm_high(first_b[p], rows_of(z, s_other))
            return direct_p - correction

        outs.append(lax.cond(col_index < 2, left_side, right_side))
    return jnp.concatenate(outs, 0)


def solution(mesh):
    return jax.shard_map(
        on_device,
        mesh=mesh,
        in_specs=(P(), P(), P(None, "mode", "col"), P(), P(), P(), P()),
        out_specs=P(("mode", "row"), "col"),
        check_vma=False,
    )
```

```python
import jax
import jax.numpy as jnp
from jax import lax
from jax.sharding import PartitionSpec as P

QMAX = 8


screen_rate = 6.0
bloch_phase = 0.7
real_amplitude = 0.15
identity_weight = 0.5

HIGHEST = lax.Precision.HIGHEST


def real_part(xr, yr, xc, yc):
    dx = xr[:, None] - xc[None, :]
    dy = yr[:, None] - yc[None, :]
    total = jnp.zeros(dx.shape, jnp.float32)
    for shift in (-1, 0, 1):
        total = total + jnp.cos(jnp.float32(bloch_phase * shift)) * jnp.exp(
            -screen_rate * ((dx - shift) ** 2 + dy * dy)
        )
    return total


HALF_PI_PARTS = (1.5703125, 4.837512969970703125e-4, 7.54978995489188216e-8)
TWO_OVER_PI = 0.6366197723675814
SIN_COEFFS = (-1.9515295891e-4, 8.3321608736e-3, -1.6666654611e-1)
COS_COEFFS = (2.443315711809948e-5, -1.388731625493765e-3, 4.166664568298827e-2)


def cos_and_negsin(theta):
    f32 = jnp.float32
    k = jnp.round(theta * f32(TWO_OVER_PI))
    r = theta
    for part in HALF_PI_PARTS:
        r = r - k * f32(part)
    z = r * r
    s = ((f32(SIN_COEFFS[0]) * z + f32(SIN_COEFFS[1])) * z + f32(SIN_COEFFS[2])) * z * r + r
    c = ((f32(COS_COEFFS[0]) * z + f32(COS_COEFFS[1])) * z + f32(COS_COEFFS[2])) * z * z
    c = c - f32(0.5) * z + f32(1.0)
    quadrant = k - f32(4.0) * jnp.floor(k * f32(0.25))
    odd = (quadrant == 1.0) | (quadrant == 3.0)
    sin_r = jnp.where(odd, c, s)
    cos_r = jnp.where(odd, s, c)
    cos_theta = jnp.where((quadrant == 1.0) | (quadrant == 2.0), -cos_r, cos_r)
    negsin_theta = jnp.where(quadrant >= 2.0, sin_r, -sin_r)
    return cos_theta, negsin_theta


def spectral_rows(xr, yr, wave, factor, pieces=1):
    theta = xr[:, None] * wave[0][None, :] + yr[:, None] * wave[1][None, :]
    cos_theta, negsin_theta = cos_and_negsin(theta)
    cos_part = cos_theta.astype(jnp.bfloat16)
    sin_part = negsin_theta.astype(jnp.bfloat16)
    cos_part, sin_part = lax.optimization_barrier((cos_part, sin_part))
    rows = cos_part.shape[0] // pieces
    out = []
    for p in range(pieces):
        spec = jnp.dot(cos_part[p * rows:(p + 1) * rows], factor[0], preferred_element_type=jnp.float32)
        out.append(spec + jnp.dot(sin_part[p * rows:(p + 1) * rows], factor[1], preferred_element_type=jnp.float32))
    return out if pieces > 1 else out[0]


def panel_rows(start, count, scale, coords, wave, factor, xc, yc, points, pieces=1):
    xr = lax.dynamic_slice_in_dim(coords[0], start, count, 0)
    yr = lax.dynamic_slice_in_dim(coords[1], start, count, 0)
    spectral = spectral_rows(xr, yr, wave, factor, pieces)
    if pieces == 1:
        spectral = [spectral]
    size = count // pieces
    out = []
    for p, spec in enumerate(spectral):
        rows = start + p * size + jnp.arange(size, dtype=jnp.int32)
        xs, ys = xr[p * size:(p + 1) * size], yr[p * size:(p + 1) * size]
        tile = real_amplitude * scale * real_part(xs, ys, xc, yc)
        diag = jnp.where(
            rows[:, None] == points[None, :], jnp.float32(identity_weight), jnp.float32(0.0)
        )
        tile, diag = lax.optimization_barrier((tile, diag))
        out.append(spec + tile + diag)
    return out if pieces > 1 else out[0]


def mm(a, b):
    return jnp.dot(a, b, precision=HIGHEST, preferred_element_type=jnp.float32)


def mm_high(a, b):
    return jnp.dot(a, b, precision=lax.Precision.HIGH, preferred_element_type=jnp.float32)


def on_device(coords, wave, col_factor, counts, blocks, inverse_first, inverse_second):
    row_count = lax.axis_size("row")
    mode_index = lax.axis_index("mode")
    row_index = lax.axis_index("row")
    col_index = lax.axis_index("col")
    block = inverse_first.shape[0]
    width = col_factor.shape[2]
    rows_dev = coords.shape[1] // (lax.axis_size("mode") * row_count)
    assert rows_dev == block and 2 * width == block
    group = mode_index * row_count + row_index

    factor = lax.all_gather(col_factor, "mode", axis=1, tiled=True)

    half = col_index % 2
    col_start = jnp.take(blocks, col_index // 2) * block + half * width
    points = col_start + jnp.arange(width, dtype=jnp.int32)
    xc = lax.dynamic_slice_in_dim(coords[0], col_start, width, 0)
    yc = lax.dynamic_slice_in_dim(coords[1], col_start, width, 0)

    own_start = group * rows_dev
    own_scale = jnp.take(counts, group).astype(jnp.float32) / QMAX
    panel_parts = panel_rows(own_start, rows_dev, own_scale, coords, wave, factor, xc, yc, points, 2)
    panel_own = jnp.concatenate(panel_parts, 0)

    pivot_block = blocks[0]
    pivot_scale = jnp.take(counts, pivot_block).astype(jnp.float32) / QMAX
    pivot_mine = panel_rows(pivot_block * block, block, pivot_scale, coords, wave, factor, xc, yc, points)

    swap = [(0, 1), (1, 0), (2, 3), (3, 2)]
    right_swap = [(2, 3), (3, 2)]
    other = lax.ppermute(panel_own, "col", swap)
    pivot_other = lax.ppermute(pivot_mine, "col", right_swap)
    first_a = [lax.ppermute(part, "col", [(0, 2), (1, 3)]) for part in panel_parts]

    s_mine = half * width
    s_other = width - s_mine
    out_cols = half * width

    def rows_of(mat, start):
        return lax.dynamic_slice_in_dim(mat, start, width, 0)

    inverse = jnp.where(col_index < 2, inverse_first, inverse_second)
    inv = lax.dynamic_slice_in_dim(inverse, out_cols, width, 1)
    direct = mm(panel_own, rows_of(inv, s_mine)) + mm(other, rows_of(inv, s_other))
    q = mm(pivot_mine, rows_of(inv, s_mine)) + mm(pivot_other, rows_of(inv, s_other))
    z = mm(inverse_first, q)
    last = lax.optimization_barrier((first_a[-1], z))[0]
    first_b = [lax.ppermute(part, "col", right_swap) for part in first_a[:-1] + [last]]

    size = rows_dev // len(panel_parts)
    outs = []
    for p in range(len(panel_parts)):
        direct_p = direct[p * size:(p + 1) * size]

        def left_side(direct_p=direct_p):
            return direct_p

        def right_side(direct_p=direct_p, p=p):
            correction = mm_high(first_a[p], rows_of(z, s_mine)) + mm_high(first_b[p], rows_of(z, s_other))
            return direct_p - correction

        outs.append(lax.cond(col_index < 2, left_side, right_side))
    head = jnp.concatenate(outs[:-1] + [direct[(len(outs) - 1) * size:]], 0)
    return lax.dynamic_update_slice_in_dim(head, outs[-1], (len(outs) - 1) * size, 0)


def solution(mesh):
    return jax.shard_map(
        on_device,
        mesh=mesh,
        in_specs=(P(), P(), P(None, "mode", "col"), P(), P(), P(), P()),
        out_specs=P(("mode", "row"), "col"),
        check_vma=False,
    )
```
